256 devices in a mesh: users: 64 (over y_lo, x, z), panel: 4 (over y_hi, core).
Axes of the slice: x: 4, y: 4 (y_hi: 2, y_lo: 2; y = y_hi * 2 + y_lo), z: 8, core: 2. Of those that a mesh axis runs over, the one named last changes fastest.
Arguments:
- user_emb0: float32 [65536, 128], P('users'), may hold values from -6 to 6
- item_base: float32 [4, 8192, 128], P('panel'), may hold values from -6 to 6
- weight_tiles: bfloat16 [64, 128, 128], replicated, may hold values from -0.02734375 to 0.02734375
- blk_user: int32 [64, 4, 384], P('users', 'panel'), may hold values from 0 to 7
- blk_item: int32 [64, 4, 384], P('users', 'panel'), may hold values from 0 to 63
- blk_weight: int32 [64, 4, 384], P('users', 'panel'), may hold values from 0 to 63
Outputs:
- user_out: float32 [65536, 128], P('users')
- item_emb: float32 [4, 8192, 128], P('panel', 'users')
The draws below stay inside these ranges and needn't reach their ends.
All inputs are finite; a program needn't handle non-finite values.
Results may differ from the reference program's by a relative error of at most 0.0036.
Values may be sent and summed in bfloat16 or wider, within the bound.
No kernel may reach another device: no remote copies, remote signals or barrier semaphores. Data moves between devices by JAX's collectives and lax.ppermute only.
A program may use at most 128 MiB of HBM per device.

```python
import math
import jax
import jax.numpy as jnp
import numpy as np
from jax import lax

E = 128
TILE = 128
UT_DEV = 8
BLK_DEV = 384
NWT = 64
USERS = 65536
ITEMS_PANEL = 8192
N_USERS = 64
N_PANEL = 4


def plant(array, own_key, smallest, top_value):
    longest = array.shape.index(max(array.shape))
    spots = []
    for shift in (0, 1):
        where = [jax.random.randint(jax.random.fold_in(own_key, axis), (), 0, length) for axis, length in enumerate(array.shape)]
        where[longest] = (where[longest] + shift) % array.shape[longest]
        spots.append(tuple(where))
    return array.at[spots[0]].set(smallest).at[spots[1]].set(top_value)


def shard_levels(rng, shape, cuts, low, top_value):
    def one(dim, shards_of):
        draws = jax.random.uniform(jax.random.fold_in(jax.random.fold_in(rng, 6), dim), (shards_of,), jnp.float32, low / len(cuts), top_value / len(cuts))
        return jnp.repeat(jnp.exp(draws), shape[dim] // shards_of).reshape((-1,) + (1,) * (len(shape) - dim - 1))

    level = one(*cuts[0])
    for cut in cuts[1:]:
        level = level * one(*cut)
    return level


def rank_bounds(amount, lean):
    loads = [(1 << 20) // math.isqrt(rank ** lean) + 1 for rank in range(1, amount + 1)]
    spread = 1 + sum(loads) // (1 << 30)
    return np.cumsum(np.array([max(1, weight // spread) for weight in loads]))


def ranked_ids(own_key, extent, amount, slope):
    listing = rank_bounds(amount, slope)
    ticket = jax.random.randint(jax.random.fold_in(own_key, 1), extent, 0, int(listing[amount - 1]))
    rank = jnp.searchsorted(jnp.asarray(listing, jnp.int32), ticket, side="right")
    return jax.random.permutation(jax.random.fold_in(own_key, 2), amount)[rank].astype(jnp.int32)


def noise(stream_key, dims, width, reach, split=(), held_as=jnp.bfloat16):
    entries = jax.random.normal(stream_key, dims, jnp.float32) * width
    if len(split) > 0:
        entries = shard_levels(stream_key, dims, split, -0.22, 0.18) * entries
    return jnp.clip(entries, min=-reach, max=reach).astype(held_as)


def setup_inputs(seed: int = 0) -> dict:
    splits = jax.random.split(jax.random.key(seed), 7)
    return {
        "user_emb0": noise(splits[0], (USERS, E), 1.0, 6.0, ((0, 64),), jnp.float32),
        "item_base": noise(splits[1], (N_PANEL, ITEMS_PANEL, E), 1.0, 6.0, ((0, 4),), jnp.float32),
        "weight_tiles": noise(splits[2], (NWT, TILE, TILE), (TILE * BLK_DEV) ** -0.5, 0.02734375),
        "blk_user": plant(jax.random.randint(splits[3], (N_USERS, N_PANEL, BLK_DEV), 0, UT_DEV), jax.random.fold_in(splits[3], 1), 0, UT_DEV - 1).astype(jnp.int32),
        "blk_item": plant(ranked_ids(splits[4], (N_USERS, N_PANEL, BLK_DEV), N_USERS, 2), jax.random.fold_in(splits[4], 3), 0, N_USERS - 1).astype(jnp.int32),
        "blk_weight": plant(jax.random.randint(splits[5], (N_USERS, N_PANEL, BLK_DEV), 0, NWT), jax.random.fold_in(splits[5], 1), 0, NWT - 1).astype(jnp.int32),
    }


teleport = 0.2


def item_terms(user_tiles, users, items, weights, weight_tiles, n_items):
    group_size = min(users.shape[0], 128)
    pieces = (users.reshape(-1, group_size), items.reshape(-1, group_size), weights.reshape(-1, group_size))

    def add_group(totals, lists):
        tiles = weight_tiles[lists[2]].astype(jnp.float32)
        rows = user_tiles[lists[0]].astype(jnp.float32)
        products = jnp.einsum("gab,gae->gbe", tiles, rows)
        return totals + jax.ops.segment_sum(products, lists[1], num_segments=n_items), None

    start = jnp.zeros((n_items, user_tiles.shape[1], user_tiles.shape[2]), jnp.float32)
    totals, unused = lax.scan(add_group, start, pieces)
    return totals


def user_terms(item_tiles, users, items, weights, weight_tiles, n_tiles):
    group_size = min(users.shape[0], 128)
    pieces = (users.reshape(-1, group_size), items.reshape(-1, group_size), weights.reshape(-1, group_size))

    def add_group(totals, lists):
        tiles = weight_tiles[lists[2]].astype(jnp.float32)
        rows = item_tiles[lists[1]].astype(jnp.float32)
        products = jnp.einsum("gab,gbe->gae", tiles, rows)
        return totals + jax.ops.segment_sum(products, lists[0], num_segments=n_tiles), None

    start = jnp.zeros((n_tiles, item_tiles.shape[1], item_tiles.shape[2]), jnp.float32)
    totals, unused = lax.scan(add_group, start, pieces)
    return totals


def reference(user_emb0, item_base, weight_tiles, blk_user, blk_item, blk_weight):
    user_bf = user_emb0.astype(jnp.bfloat16).reshape(N_USERS, UT_DEV, TILE, E)

    def item_device(totals, device):
        user_local = device[0]

        def one_panel(lists):
            return item_terms(user_local, lists[0], lists[1], lists[2], weight_tiles, N_USERS)

        terms = lax.map(one_panel, (device[1], device[2], device[3]))
        return totals + terms, None

    start = jnp.zeros((N_PANEL, N_USERS, TILE, E), jnp.float32)
    item_sum, unused = lax.scan(item_device, start, (user_bf, blk_user, blk_item, blk_weight))
    item_emb = (1.0 - teleport) * item_sum.reshape(N_PANEL, N_USERS * TILE, E) + teleport * item_base
    item_bf = item_emb.astype(jnp.bfloat16).reshape(N_PANEL, N_USERS, TILE, E)

    def user_device(device):
        def one_panel(lists):
            return user_terms(lists[0], lists[1], lists[2], lists[3], weight_tiles, UT_DEV)

        terms = lax.map(one_panel, (item_bf, device[0], device[1], device[2]))
        return jnp.sum(terms, axis=0)

    user_sum = lax.map(user_device, (blk_user, blk_item, blk_weight))
    user_out = (1.0 - teleport) * user_sum.reshape(USERS, E) + teleport * user_emb0
    return user_out, item_emb
```

```python
import jax
import jax.numpy as jnp
from jax import lax
from jax.experimental import pallas as pl
from jax.experimental.pallas import tpu as pltpu
from jax.sharding import Mesh
from jax.sharding import PartitionSpec as P

teleport = 0.2

USER_AXES = ("ylo", "x", "z")
PANEL_AXES = ("yhi", "core")


def block_sum_kernel(a_index_ref, b_index_ref, out_index_ref, a_ref, b_ref, o_ref):
    o_ref[...] = jnp.zeros(o_ref.shape, o_ref.dtype)
    n_blocks = a_index_ref.shape[0]

    def body(k, carry):
        a = a_ref[a_index_ref[k]]
        b = b_ref[b_index_ref[k]]
        o_ref[out_index_ref[k]] += jnp.dot(a, b, preferred_element_type=jnp.float32)
        return carry

    lax.fori_loop(0, n_blocks, body, 0)


def block_sums(lists, a_tiles, b_tiles, n_out):
    tile = a_tiles.shape[1]
    width = b_tiles.shape[2]
    return pl.pallas_call(
        block_sum_kernel,
        grid_spec=pltpu.PrefetchScalarGridSpec(
            num_scalar_prefetch=3,
            grid=(1,),
            in_specs=[
                pl.BlockSpec(a_tiles.shape, lambda i, *_: (0, 0, 0)),
                pl.BlockSpec(b_tiles.shape, lambda i, *_: (0, 0, 0)),
            ],
            out_specs=pl.BlockSpec((n_out, tile, width), lambda i, *_: (0, 0, 0)),
        ),
        out_shape=jax.ShapeDtypeStruct((n_out, tile, width), jnp.float32),
    )(lists[0], lists[1], lists[2], a_tiles, b_tiles)


def ring_reduce_scatter(x, axis, n):
    i = lax.axis_index(axis)
    h = x.shape[1] // 2
    xl, xr = x[:, :h], x[:, h:]
    right = [(j, (j + 1) % n) for j in range(n)]
    left = [(j, (j - 1) % n) for j in range(n)]
    bl = lax.dynamic_index_in_dim(xl, (i - 1) % n, 0, keepdims=False)
    br = lax.dynamic_index_in_dim(xr, (i + 1) % n, 0, keepdims=False)
    for s in range(n - 1):
        rl = lax.ppermute(bl, axis, right)
        rr = lax.ppermute(br, axis, left)
        bl = rl + lax.dynamic_index_in_dim(xl, (i - s - 2) % n, 0, keepdims=False)
        br = rr + lax.dynamic_index_in_dim(xr, (i + s + 2) % n, 0, keepdims=False)
    return jnp.concatenate([bl, br], 0)


def ring_all_gather(x, axis, n):
    i = lax.axis_index(axis)
    h = x.shape[0] // 2
    right = [(j, (j + 1) % n) for j in range(n)]
    left = [(j, (j - 1) % n) for j in range(n)]
    out = jnp.zeros((n,) + x.shape, x.dtype)
    out = lax.dynamic_update_index_in_dim(out, x, i, 0)
    bl, br = x[:h], x[h:]
    zeros = (0,) * (x.ndim - 1)
    for s in range(n - 1):
        bl = lax.ppermute(bl, axis, right)
        br = lax.ppermute(br, axis, left)
        out = lax.dynamic_update_slice(out, bl[None], ((i - s - 1) % n, 0) + zeros)
        out = lax.dynamic_update_slice(out, br[None], ((i + s + 1) % n, h) + zeros)
    return out


def per_device(user_emb0, item_base, weight_tiles, blk_user, blk_item, blk_weight, *, sizes):
    n_ylo, n_x, n_z, n_yhi, n_core = sizes
    n_users = n_ylo * n_x * n_z
    tile_rows = weight_tiles.shape[1]
    width = user_emb0.shape[1]
    user_tiles = user_emb0.astype(jnp.bfloat16).reshape(-1, tile_rows, width)
    n_user_tiles = user_tiles.shape[0]
    lists = (blk_user.reshape(-1), blk_item.reshape(-1), blk_weight.reshape(-1))
    weights_t = jnp.swapaxes(weight_tiles, 1, 2)

    partial = block_sums(
        (lists[2], lists[0], lists[1]), weights_t, user_tiles, n_users
    )
    x = partial.reshape(n_ylo, n_x, n_z, tile_rows, width)
    x = x.transpose(2, 1, 0, 3, 4).reshape(n_z, n_x * n_ylo * tile_rows, width)
    x = ring_reduce_scatter(x, "z", n_z)
    x = ring_reduce_scatter(x.reshape(n_x, n_ylo * tile_rows, width), "x", n_x)
    own_sum = ring_reduce_scatter(x.reshape(n_ylo, tile_rows, width), "ylo", n_ylo)

    position = lax.axis_index(USER_AXES)
    own_base = lax.dynamic_slice_in_dim(item_base[0], position * tile_rows, tile_rows, 0)
    own_emb = (1.0 - teleport) * own_sum + teleport * own_base
    own_bf = own_emb.astype(jnp.bfloat16)
    spread = jnp.broadcast_to(own_bf[None], (n_users, tile_rows, width))
    item_tiles = lax.all_to_all(spread, USER_AXES, 0, 0, tiled=True)

    user_part = block_sums(
        (lists[2], lists[1], lists[0]), weight_tiles, item_tiles, n_user_tiles
    )
    y = user_part.reshape(n_core, -1, width)
    y = ring_reduce_scatter(y, "core", n_core)
    y = ring_reduce_scatter(y.reshape(n_yhi, -1, width), "yhi", n_yhi)
    y = ring_all_gather(y, "yhi", n_yhi).reshape(-1, width)
    y = ring_all_gather(y, "core", n_core).reshape(-1, width)
    user_out = (1.0 - teleport) * y + teleport * user_emb0
    return (user_out, own_emb[None])


def solution(mesh):
    import functools

    sizes = (2, 4, 8, 2, 2)
    fine = Mesh(mesh.devices.reshape(sizes), USER_AXES + PANEL_AXES)
    placed = (
        P(USER_AXES, None),
        P(PANEL_AXES, None, None),
        P(),
        P(USER_AXES, PANEL_AXES, None),
        P(USER_AXES, PANEL_AXES, None),
        P(USER_AXES, PANEL_AXES, None),
    )
    return jax.shard_map(
        functools.partial(per_device, sizes=sizes),
        mesh=fine,
        in_specs=placed,
        out_specs=(P(USER_AXES, None), P(PANEL_AXES, USER_AXES, None)),
        check_vma=False,
    )
```

```python
import jax
import jax.numpy as jnp
from jax import lax
from jax.experimental import pallas as pl
from jax.experimental.pallas import tpu as pltpu
from jax.sharding import Mesh
from jax.sharding import PartitionSpec as P

teleport = 0.2

USER_AXES = ("ylo", "x", "z")
PANEL_AXES = ("yhi", "core")


def block_sum_kernel(a_index_ref, b_index_ref, out_index_ref, a_ref, b_ref, o_ref):
    o_ref[...] = jnp.zeros(o_ref.shape, o_ref.dtype)
    n_blocks = a_index_ref.shape[0]

    def body(k, carry):
        a = a_ref[a_index_ref[k]]
        b = b_ref[b_index_ref[k]]
        o_ref[out_index_ref[k]] += jnp.dot(a, b, preferred_element_type=jnp.float32)
        return carry

    lax.fori_loop(0, n_blocks, body, 0, unroll=8)


def block_sums(lists, a_tiles, b_tiles, n_out):
    tile = a_tiles.shape[1]
    width = b_tiles.shape[2]
    return pl.pallas_call(
        block_sum_kernel,
        grid_spec=pltpu.PrefetchScalarGridSpec(
            num_scalar_prefetch=3,
            grid=(1,),
            in_specs=[
                pl.BlockSpec(a_tiles.shape, lambda i, *_: (0, 0, 0)),
                pl.BlockSpec(b_tiles.shape, lambda i, *_: (0, 0, 0)),
            ],
            out_specs=pl.BlockSpec((n_out, tile, width), lambda i, *_: (0, 0, 0)),
        ),
        out_shape=jax.ShapeDtypeStruct((n_out, tile, width), jnp.float32),
    )(lists[0], lists[1], lists[2], a_tiles, b_tiles)


def ring_reduce_scatter(x, axis, n):
    i = lax.axis_index(axis)
    h = x.shape[1] // 2
    xl, xr = x[:, :h], x[:, h:]
    right = [(j, (j + 1) % n) for j in range(n)]
    left = [(j, (j - 1) % n) for j in range(n)]
    bl = lax.dynamic_index_in_dim(xl, (i - 1) % n, 0, keepdims=False)
    br = lax.dynamic_index_in_dim(xr, (i + 1) % n, 0, keepdims=False)
    for s in range(n - 1):
        rl = lax.ppermute(bl, axis, right)
        rr = lax.ppermute(br, axis, left)
        bl = rl + lax.dynamic_index_in_dim(xl, (i - s - 2) % n, 0, keepdims=False)
        br = rr + lax.dynamic_index_in_dim(xr, (i + s + 2) % n, 0, keepdims=False)
    return jnp.concatenate([bl, br], 0)


def ring_all_gather(x, axis, n):
    i = lax.axis_index(axis)
    h = x.shape[0] // 2
    right = [(j, (j + 1) % n) for j in range(n)]
    left = [(j, (j - 1) % n) for j in range(n)]
    out = jnp.zeros((n,) + x.shape, x.dtype)
    out = lax.dynamic_update_index_in_dim(out, x, i, 0)
    bl, br = x[:h], x[h:]
    zeros = (0,) * (x.ndim - 1)
    for s in range(n - 1):
        bl = lax.ppermute(bl, axis, right)
        br = lax.ppermute(br, axis, left)
        out = lax.dynamic_update_slice(out, bl[None], ((i - s - 1) % n, 0) + zeros)
        out = lax.dynamic_update_slice(out, br[None], ((i + s + 1) % n, h) + zeros)
    return out


def per_device(user_emb0, item_base, weight_tiles, blk_user, blk_item, blk_weight, *, sizes):
    n_ylo, n_x, n_z, n_yhi, n_core = sizes
    n_users = n_ylo * n_x * n_z
    tile_rows = weight_tiles.shape[1]
    width = user_emb0.shape[1]
    user_tiles = user_emb0.astype(jnp.bfloat16).reshape(-1, tile_rows, width)
    n_user_tiles = user_tiles.shape[0]
    lists = (blk_user.reshape(-1), blk_item.reshape(-1), blk_weight.reshape(-1))
    weights_t = jnp.swapaxes(weight_tiles, 1, 2)

    partial = block_sums(
        (lists[2], lists[0], lists[1]), weights_t, user_tiles, n_users
    )
    x = partial.reshape(n_ylo, n_x, n_z, tile_rows, width)
    x = x.transpose(2, 1, 0, 3, 4).reshape(n_z, n_x * n_ylo * tile_rows, width)
    x = ring_reduce_scatter(x, "z", n_z)
    x = ring_reduce_scatter(x.reshape(n_x, n_ylo * tile_rows, width), "x", n_x)
    own_sum = ring_reduce_scatter(x.reshape(n_ylo, tile_rows, width), "ylo", n_ylo)

    position = lax.axis_index(USER_AXES)
    own_base = lax.dynamic_slice_in_dim(item_base[0], position * tile_rows, tile_rows, 0)
    own_emb = (1.0 - teleport) * own_sum + teleport * own_base
    own_bf = own_emb.astype(jnp.bfloat16)
    spread = jnp.broadcast_to(own_bf[None], (n_users, tile_rows, width))
    item_tiles = lax.all_to_all(spread, USER_AXES, 0, 0, tiled=True)

    user_part = block_sums(
        (lists[2], lists[1], lists[0]), weight_tiles, item_tiles, n_user_tiles
    )
    y = user_part.reshape(n_core, -1, width)
    y = ring_reduce_scatter(y, "core", n_core)
    y = ring_reduce_scatter(y.reshape(n_yhi, -1, width), "yhi", n_yhi)
    y = ring_all_gather(y, "yhi", n_yhi).reshape(-1, width)
    y = ring_all_gather(y, "core", n_core).reshape(-1, width)
    user_out = (1.0 - teleport) * y + teleport * user_emb0
    return (user_out, own_emb[None])


def solution(mesh):
    import functools

    sizes = (2, 4, 8, 2, 2)
    fine = Mesh(mesh.devices.reshape(sizes), USER_AXES + PANEL_AXES)
    placed = (
        P(USER_AXES, None),
        P(PANEL_AXES, None, None),
        P(),
        P(USER_AXES, PANEL_AXES, None),
        P(USER_AXES, PANEL_AXES, None),
        P(USER_AXES, PANEL_AXES, None),
    )
    return jax.shard_map(
        functools.partial(per_device, sizes=sizes),
        mesh=fine,
        in_specs=placed,
        out_specs=(P(USER_AXES, None), P(PANEL_AXES, USER_AXES, None)),
        check_vma=False,
    )
```

```python
import jax
import jax.numpy as jnp
from jax import lax
from jax.experimental import pallas as pl
from jax.experimental.pallas import tpu as pltpu
from jax.sharding import Mesh
from jax.sharding import PartitionSpec as P

teleport = 0.2

USER_AXES = ("ylo", "x", "z")
PANEL_AXES = ("yhi", "core")


def block_sum_kernel(index_ref, a_ref, b_ref, o_ref):
    o_ref[...] = jnp.zeros(o_ref.shape, o_ref.dtype)
    n_blocks = index_ref.shape[0] // 3

    def body(k, carry):
        a = a_ref[index_ref[k]]
        b = b_ref[index_ref[n_blocks + k]]
        o_ref[index_ref[2 * n_blocks + k]] += jnp.dot(a, b, preferred_element_type=jnp.float32)
        return carry

    lax.fori_loop(0, n_blocks, body, 0, unroll=8)


def block_sums(index, a_tiles, b_tiles, n_out):
    tile = a_tiles.shape[1]
    width = b_tiles.shape[2]
    return pl.pallas_call(
        block_sum_kernel,
        grid_spec=pltpu.PrefetchScalarGridSpec(
            num_scalar_prefetch=1,
            grid=(1,),
            in_specs=[
                pl.BlockSpec(a_tiles.shape, lambda i, *_: (0, 0, 0)),
                pl.BlockSpec(b_tiles.shape, lambda i, *_: (0, 0, 0)),
            ],
            out_specs=pl.BlockSpec((n_out, tile, width), lambda i, *_: (0, 0, 0)),
        ),
        out_shape=jax.ShapeDtypeStruct((n_out, tile, width), jnp.float32),
    )(index, a_tiles, b_tiles)


def ring_reduce_scatter(x, axis, n):
    i = lax.axis_index(axis)
    h = x.shape[1] // 2
    xl, xr = x[:, :h], x[:, h:]
    right = [(j, (j + 1) % n) for j in range(n)]
    left = [(j, (j - 1) % n) for j in range(n)]
    bl = lax.dynamic_index_in_dim(xl, (i - 1) % n, 0, keepdims=False)
    br = lax.dynamic_index_in_dim(xr, (i + 1) % n, 0, keepdims=False)
    for s in range(n - 1):
        rl = lax.ppermute(bl, axis, right)
        rr = lax.ppermute(br, axis, left)
        bl = rl + lax.dynamic_index_in_dim(xl, (i - s - 2) % n, 0, keepdims=False)
        br = rr + lax.dynamic_index_in_dim(xr, (i + s + 2) % n, 0, keepdims=False)
    return jnp.concatenate([bl, br], 0)


def ring_all_gather(x, axis, n):
    i = lax.axis_index(axis)
    h = x.shape[0] // 2
    right = [(j, (j + 1) % n) for j in range(n)]
    left = [(j, (j - 1) % n) for j in range(n)]
    out = jnp.zeros((n,) + x.shape, x.dtype)
    out = lax.dynamic_update_index_in_dim(out, x, i, 0)
    bl, br = x[:h], x[h:]
    zeros = (0,) * (x.ndim - 1)
    for s in range(n - 1):
        bl = lax.ppermute(bl, axis, right)
        br = lax.ppermute(br, axis, left)
        out = lax.dynamic_update_slice(out, bl[None], ((i - s - 1) % n, 0) + zeros)
        out = lax.dynamic_update_slice(out, br[None], ((i + s + 1) % n, h) + zeros)
    return out


def per_device(user_emb0, item_base, weight_tiles, blk_user, blk_item, blk_weight, *, sizes):
    n_ylo, n_x, n_z, n_yhi, n_core = sizes
    n_users = n_ylo * n_x * n_z
    tile_rows = weight_tiles.shape[1]
    width = user_emb0.shape[1]
    user_tiles = user_emb0.astype(jnp.bfloat16).reshape(-1, tile_rows, width)
    n_user_tiles = user_tiles.shape[0]
    users_list = blk_user.reshape(-1)
    items_list = blk_item.reshape(-1)
    weights_list = blk_weight.reshape(-1)
    weights_t = jnp.swapaxes(weight_tiles, 1, 2)

    item_ylo = items_list // (n_x * n_z)
    item_x = (items_list // n_z) % n_x
    item_z = items_list % n_z
    item_slot = (item_z * n_ylo + item_ylo) * n_x + item_x
    item_index = jnp.concatenate([weights_list, users_list, item_slot])
    partial = block_sums(item_index, weights_t, user_tiles, n_users)
    x = partial.reshape(n_z, n_ylo * n_x * tile_rows, width)
    x = ring_reduce_scatter(x, "z", n_z)
    x = lax.all_to_all(x.reshape(n_ylo * n_x, tile_rows, width), ("ylo", "x"), 0, 0, tiled=True)
    own_sum = x.sum(0)

    position = lax.axis_index(USER_AXES)
    own_base = lax.dynamic_slice_in_dim(item_base[0], position * tile_rows, tile_rows, 0)
    own_emb = (1.0 - teleport) * own_sum + teleport * own_base
    own_bf = own_emb.astype(jnp.bfloat16)
    t = lax.all_to_all(jnp.broadcast_to(own_bf[None], (n_z, tile_rows, width)), "z", 0, 0, tiled=True)
    t = jnp.broadcast_to(t[None], (n_ylo * n_x, n_z, tile_rows, width))
    t = lax.all_to_all(t, ("ylo", "x"), 0, 0, tiled=True)
    item_tiles = t.reshape(n_users, tile_rows, width)

    user_index = jnp.concatenate([weights_list, items_list, users_list])
    user_part = block_sums(user_index, weight_tiles, item_tiles, n_user_tiles)
    y = user_part.reshape(n_core, -1, width)
    y = ring_reduce_scatter(y, "core", n_core)
    y = ring_reduce_scatter(y.reshape(n_yhi, -1, width), "yhi", n_yhi)
    y = ring_all_gather(y, "yhi", n_yhi).reshape(-1, width)
    y = ring_all_gather(y, "core", n_core).reshape(-1, width)
    user_out = (1.0 - teleport) * y + teleport * user_emb0
    return (user_out, own_emb[None])


def solution(mesh):
    import functools

    sizes = (2, 4, 8, 2, 2)
    fine = Mesh(mesh.devices.reshape(sizes), USER_AXES + PANEL_AXES)
    placed = (
        P(USER_AXES, None),
        P(PANEL_AXES, None, None),
        P(),
        P(USER_AXES, PANEL_AXES, None),
        P(USER_AXES, PANEL_AXES, None),
        P(USER_AXES, PANEL_AXES, None),
    )
    return jax.shard_map(
        functools.partial(per_device, sizes=sizes),
        mesh=fine,
        in_specs=placed,
        out_specs=(P(USER_AXES, None), P(PANEL_AXES, USER_AXES, None)),
        check_vma=False,
    )
```

```python
import jax
import jax.numpy as jnp
from jax import lax
from jax.experimental import pallas as pl
from jax.experimental.pallas import tpu as pltpu
from jax.sharding import Mesh
from jax.sharding import PartitionSpec as P

teleport = 0.2

USER_AXES = ("ylo", "x", "z")
PANEL_AXES = ("yhi", "core")


def block_sum_kernel(index_ref, a_ref, b_ref, o_ref, *, b_transposed):
    o_ref[...] = jnp.zeros(o_ref.shape, o_ref.dtype)
    n_blocks = index_ref.shape[0] // 3

    def body(k, carry):
        a = a_ref[index_ref[k]]
        b = b_ref[index_ref[n_blocks + k]]
        contract = ((1,), (1,) if b_transposed else (0,))
        o_ref[index_ref[2 * n_blocks + k]] += lax.dot_general(
            a, b, (contract, ((), ())), preferred_element_type=jnp.float32
        )
        return carry

    lax.fori_loop(0, n_blocks, body, 0, unroll=8)


def block_sums(index, a_tiles, b_tiles, n_out, b_transposed=False):
    import functools

    tile = a_tiles.shape[1]
    width = b_tiles.shape[1] if b_transposed else b_tiles.shape[2]
    return pl.pallas_call(
        functools.partial(block_sum_kernel, b_transposed=b_transposed),
        grid_spec=pltpu.PrefetchScalarGridSpec(
            num_scalar_prefetch=1,
            grid=(1,),
            in_specs=[
                pl.BlockSpec(a_tiles.shape, lambda i, *_: (0, 0, 0)),
                pl.BlockSpec(b_tiles.shape, lambda i, *_: (0, 0, 0)),
            ],
            out_specs=pl.BlockSpec((n_out, tile, width), lambda i, *_: (0, 0, 0)),
        ),
        out_shape=jax.ShapeDtypeStruct((n_out, tile, width), jnp.float32),
    )(index, a_tiles, b_tiles)


def ring_reduce_scatter(x, axis, n):
    h = x.shape[1] // 2
    return jnp.concatenate(ring_reduce_scatter_halves(x[:, :h], x[:, h:], axis, n), 0)


def ring_reduce_scatter_halves(xl, xr, axis, n):
    i = lax.axis_index(axis)
    right = [(j, (j + 1) % n) for j in range(n)]
    left = [(j, (j - 1) % n) for j in range(n)]
    bl = lax.dynamic_index_in_dim(xl, (i - 1) % n, 0, keepdims=False)
    br = lax.dynamic_index_in_dim(xr, (i + 1) % n, 0, keepdims=False)
    for s in range(n - 1):
        rl = lax.ppermute(bl, axis, right)
        rr = lax.ppermute(br, axis, left)
        bl = rl + lax.dynamic_index_in_dim(xl, (i - s - 2) % n, 0, keepdims=False)
        br = rr + lax.dynamic_index_in_dim(xr, (i + s + 2) % n, 0, keepdims=False)
    return bl, br


def ring_all_gather(x, axis, n):
    i = lax.axis_index(axis)
    h = x.shape[0] // 2
    right = [(j, (j + 1) % n) for j in range(n)]
    left = [(j, (j - 1) % n) for j in range(n)]
    out = jnp.zeros((n,) + x.shape, x.dtype)
    out = lax.dynamic_update_index_in_dim(out, x, i, 0)
    bl, br = x[:h], x[h:]
    zeros = (0,) * (x.ndim - 1)
    for s in range(n - 1):
        bl = lax.ppermute(bl, axis, right)
        br = lax.ppermute(br, axis, left)
        out = lax.dynamic_update_slice(out, bl[None], ((i - s - 1) % n, 0) + zeros)
        out = lax.dynamic_update_slice(out, br[None], ((i + s + 1) % n, h) + zeros)
    return out


def per_device(user_emb0, item_base, weight_tiles, blk_user, blk_item, blk_weight, *, sizes):
    n_ylo, n_x, n_z, n_yhi, n_core = sizes
    n_users = n_ylo * n_x * n_z
    tile_rows = weight_tiles.shape[1]
    width = user_emb0.shape[1]
    n_user_tiles = user_emb0.shape[0] // tile_rows
    user_tiles_t = jnp.swapaxes(user_emb0.astype(jnp.bfloat16).reshape(-1, tile_rows, width), 1, 2)
    users_list = blk_user.reshape(-1)
    items_list = blk_item.reshape(-1)
    weights_list = blk_weight.reshape(-1)

    item_ylo = items_list // (n_x * n_z)
    item_x = (items_list // n_z) % n_x
    item_z = items_list % n_z
    item_slot = (item_ylo * n_z + item_z) * n_x + item_x
    item_index = jnp.concatenate([users_list, weights_list, item_slot])
    partial_t = block_sums(item_index, user_tiles_t, weight_tiles, n_users)
    halves = partial_t.reshape(n_ylo, n_z, n_x * tile_rows, width)
    bl, br = ring_reduce_scatter_halves(halves[0], halves[1], "z", n_z)
    x = jnp.concatenate([bl, br], 0).reshape(n_ylo * n_x, tile_rows, width)
    x = lax.all_to_all(x, ("ylo", "x"), 0, 0, tiled=True)
    own_sum = x.sum(0).T

    position = lax.axis_index(USER_AXES)
    own_base = lax.dynamic_slice_in_dim(item_base[0], position * tile_rows, tile_rows, 0)
    own_emb = (1.0 - teleport) * own_sum + teleport * own_base
    own_bf_t = own_emb.astype(jnp.bfloat16).T
    t = lax.all_to_all(jnp.broadcast_to(own_bf_t[None], (n_z, width, tile_rows)), "z", 0, 0, tiled=True)
    t = jnp.broadcast_to(t[None], (n_ylo * n_x, n_z, width, tile_rows))
    t = lax.all_to_all(t, ("ylo", "x"), 0, 0, tiled=True)
    item_tiles_t = t.reshape(n_users, width, tile_rows)

    user_index = jnp.concatenate([weights_list, items_list, users_list])
    user_part = block_sums(user_index, weight_tiles, item_tiles_t, n_user_tiles, b_transposed=True)
    y = user_part.reshape(n_core, -1, width)
    y = ring_reduce_scatter(y, "core", n_core)
    y = ring_reduce_scatter(y.reshape(n_yhi, -1, width), "yhi", n_yhi)
    y = ring_all_gather(y, "yhi", n_yhi).reshape(-1, width)
    y = ring_all_gather(y, "core", n_core).reshape(-1, width)
    user_out = (1.0 - teleport) * y + teleport * user_emb0
    return (user_out, own_emb[None])


def solution(mesh):
    import functools

    sizes = (2, 4, 8, 2, 2)
    fine = Mesh(mesh.devices.reshape(sizes), USER_AXES + PANEL_AXES)
    placed = (
        P(USER_AXES, None),
        P(PANEL_AXES, None, None),
        P(),
        P(USER_AXES, PANEL_AXES, None),
        P(USER_AXES, PANEL_AXES, None),
        P(USER_AXES, PANEL_AXES, None),
    )
    return jax.shard_map(
        functools.partial(per_device, sizes=sizes),
        mesh=fine,
        in_specs=placed,
        out_specs=(P(USER_AXES, None), P(PANEL_AXES, USER_AXES, None)),
        check_vma=False,
    )
```

```python
import jax
import jax.numpy as jnp
from jax import lax
from jax.experimental import pallas as pl
from jax.experimental.pallas import tpu as pltpu
from jax.sharding import Mesh
from jax.sharding import PartitionSpec as P

teleport = 0.2

USER_AXES = ("ylo", "x", "z")
PANEL_AXES = ("yhi", "core")


def block_sum_kernel(index_ref, a_ref, b_ref, o_ref, *, b_transposed):
    o_ref[...] = jnp.zeros(o_ref.shape, o_ref.dtype)
    n_blocks = index_ref.shape[0] // 3

    def body(k, carry):
        a = a_ref[index_ref[k]]
        b = b_ref[index_ref[n_blocks + k]]
        contract = ((1,), (1,) if b_transposed else (0,))
        o_ref[index_ref[2 * n_blocks + k]] += lax.dot_general(
            a, b, (contract, ((), ())), preferred_element_type=jnp.float32
        )
        return carry

    lax.fori_loop(0, n_blocks, body, 0, unroll=8)


def block_sums(index, a_tiles, b_tiles, n_out, b_transposed=False):
    import functools

    tile = a_tiles.shape[1]
    width = b_tiles.shape[1] if b_transposed else b_tiles.shape[2]
    return pl.pallas_call(
        functools.partial(block_sum_kernel, b_transposed=b_transposed),
        grid_spec=pltpu.PrefetchScalarGridSpec(
            num_scalar_prefetch=1,
            grid=(1,),
            in_specs=[
                pl.BlockSpec(a_tiles.shape, lambda i, *_: (0, 0, 0)),
                pl.BlockSpec(b_tiles.shape, lambda i, *_: (0, 0, 0)),
            ],
            out_specs=pl.BlockSpec((n_out, tile, width), lambda i, *_: (0, 0, 0)),
        ),
        out_shape=jax.ShapeDtypeStruct((n_out, tile, width), jnp.float32),
    )(index, a_tiles, b_tiles)


def ring_reduce_scatter(x, axis, n):
    h = x.shape[1] // 2
    return jnp.concatenate(ring_reduce_scatter_halves(x[:, :h], x[:, h:], axis, n), 0)


def ring_reduce_scatter_halves(xl, xr, axis, n):
    i = lax.axis_index(axis)
    right = [(j, (j + 1) % n) for j in range(n)]
    left = [(j, (j - 1) % n) for j in range(n)]
    bl = lax.dynamic_index_in_dim(xl, (i - 1) % n, 0, keepdims=False)
    br = lax.dynamic_index_in_dim(xr, (i + 1) % n, 0, keepdims=False)
    for s in range(n - 1):
        rl = lax.ppermute(bl, axis, right)
        rr = lax.ppermute(br, axis, left)
        bl = rl + lax.dynamic_index_in_dim(xl, (i - s - 2) % n, 0, keepdims=False)
        br = rr + lax.dynamic_index_in_dim(xr, (i + s + 2) % n, 0, keepdims=False)
    return bl, br


def ring_all_gather(x, axis, n):
    i = lax.axis_index(axis)
    h = x.shape[0] // 2
    right = [(j, (j + 1) % n) for j in range(n)]
    left = [(j, (j - 1) % n) for j in range(n)]
    out = jnp.zeros((n,) + x.shape, x.dtype)
    out = lax.dynamic_update_index_in_dim(out, x, i, 0)
    bl, br = x[:h], x[h:]
    zeros = (0,) * (x.ndim - 1)
    for s in range(n - 1):
        bl = lax.ppermute(bl, axis, right)
        br = lax.ppermute(br, axis, left)
        out = lax.dynamic_update_slice(out, bl[None], ((i - s - 1) % n, 0) + zeros)
        out = lax.dynamic_update_slice(out, br[None], ((i + s + 1) % n, h) + zeros)
    return out


def per_device(user_emb0, item_base, weight_tiles, blk_user, blk_item, blk_weight, *, sizes):
    n_ylo, n_x, n_z, n_yhi, n_core = sizes
    n_users = n_ylo * n_x * n_z
    tile_rows = weight_tiles.shape[1]
    width = user_emb0.shape[1]
    n_user_tiles = user_emb0.shape[0] // tile_rows
    user_tiles_t = jnp.swapaxes(user_emb0.astype(jnp.bfloat16).reshape(-1, tile_rows, width), 1, 2)
    users_list = blk_user.reshape(-1)
    items_list = blk_item.reshape(-1)
    weights_list = blk_weight.reshape(-1)

    item_ylo = items_list // (n_x * n_z)
    item_x = (items_list // n_z) % n_x
    item_z = items_list % n_z
    item_slot = (item_ylo * n_z + item_z) * n_x + item_x
    item_index = jnp.concatenate([users_list, weights_list, item_slot])
    partial_t = block_sums(item_index, user_tiles_t, weight_tiles, n_users)
    half = tile_rows // 2
    pt = partial_t.reshape(n_ylo, n_z, n_x, tile_rows, width)
    late = pt[..., half:, :].transpose(0, 2, 1, 3, 4).reshape(n_ylo * n_x, n_z, half, width)
    late = lax.all_to_all(late, ("ylo", "x"), 0, 0, tiled=True).sum(0)
    early = pt[..., :half, :].reshape(n_ylo, n_z, n_x * half, width)
    bl, br = ring_reduce_scatter_halves(early[0], early[1], "z", n_z)
    early = jnp.concatenate([bl, br], 0).reshape(n_ylo * n_x, half, width)
    early = lax.all_to_all(early, ("ylo", "x"), 0, 0, tiled=True).sum(0)
    late = lax.all_to_all(late, "z", 0, 0, tiled=True).sum(0)
    own_sum = jnp.concatenate([early, late], 0).T

    position = lax.axis_index(USER_AXES)
    own_base = lax.dynamic_slice_in_dim(item_base[0], position * tile_rows, tile_rows, 0)
    own_emb = (1.0 - teleport) * own_sum + teleport * own_base
    own_bf_t = own_emb.astype(jnp.bfloat16).T
    t = lax.all_to_all(jnp.broadcast_to(own_bf_t[None], (n_z, width, tile_rows)), "z", 0, 0, tiled=True)
    t = jnp.broadcast_to(t[None], (n_ylo * n_x, n_z, width, tile_rows))
    t = lax.all_to_all(t, ("ylo", "x"), 0, 0, tiled=True)
    item_tiles_t = t.reshape(n_users, width, tile_rows)

    user_index = jnp.concatenate([weights_list, items_list, users_list])
    user_part = block_sums(user_index, weight_tiles, item_tiles_t, n_user_tiles, b_transposed=True)
    y = user_part.reshape(n_core, -1, width)
    y = ring_reduce_scatter(y, "core", n_core)
    y = ring_reduce_scatter(y.reshape(n_yhi, -1, width), "yhi", n_yhi)
    y = ring_all_gather(y, "yhi", n_yhi).reshape(-1, width)
    y = ring_all_gather(y, "core", n_core).reshape(-1, width)
    user_out = (1.0 - teleport) * y + teleport * user_emb0
    return (user_out, own_emb[None])


def solution(mesh):
    import functools

    sizes = (2, 4, 8, 2, 2)
    fine = Mesh(mesh.devices.reshape(sizes), USER_AXES + PANEL_AXES)
    placed = (
        P(USER_AXES, None),
        P(PANEL_AXES, None, None),
        P(),
        P(USER_AXES, PANEL_AXES, None),
        P(USER_AXES, PANEL_AXES, None),
        P(USER_AXES, PANEL_AXES, None),
    )
    return jax.shard_map(
        functools.partial(per_device, sizes=sizes),
        mesh=fine,
        in_specs=placed,
        out_specs=(P(USER_AXES, None), P(PANEL_AXES, USER_AXES, None)),
        check_vma=False,
    )
```

```python
import jax
import jax.numpy as jnp
from jax import lax
from jax.experimental import pallas as pl
from jax.experimental.pallas import tpu as pltpu
from jax.sharding import Mesh
from jax.sharding import PartitionSpec as P

teleport = 0.2

USER_AXES = ("ylo", "x", "z")
PANEL_AXES = ("yhi", "core")


def block_sum_kernel(index_ref, a_ref, b_ref, o_ref, *, b_transposed):
    o_ref[...] = jnp.zeros(o_ref.shape, o_ref.dtype)
    n_blocks = index_ref.shape[0] // 3

    def body(k, carry):
        a = a_ref[index_ref[k]]
        b = b_ref[index_ref[n_blocks + k]]
        contract = ((1,), (1,) if b_transposed else (0,))
        o_ref[index_ref[2 * n_blocks + k]] += lax.dot_general(
            a, b, (contract, ((), ())), preferred_element_type=jnp.float32
        )
        return carry

    lax.fori_loop(0, n_blocks, body, 0, unroll=16)


def block_sums(index, a_tiles, b_tiles, n_out, b_transposed=False):
    import functools

    tile = a_tiles.shape[1]
    width = b_tiles.shape[1] if b_transposed else b_tiles.shape[2]
    return pl.pallas_call(
        functools.partial(block_sum_kernel, b_transposed=b_transposed),
        grid_spec=pltpu.PrefetchScalarGridSpec(
            num_scalar_prefetch=1,
            grid=(1,),
            in_specs=[
                pl.BlockSpec(a_tiles.shape, lambda i, *_: (0, 0, 0)),
                pl.BlockSpec(b_tiles.shape, lambda i, *_: (0, 0, 0)),
            ],
            out_specs=pl.BlockSpec((n_out, tile, width), lambda i, *_: (0, 0, 0)),
        ),
        out_shape=jax.ShapeDtypeStruct((n_out, tile, width), jnp.float32),
    )(index, a_tiles, b_tiles)


def ring_reduce_scatter(x, axis, n):
    h = x.shape[1] // 2
    return jnp.concatenate(ring_reduce_scatter_halves(x[:, :h], x[:, h:], axis, n), 0)


def ring_reduce_scatter_halves(xl, xr, axis, n):
    i = lax.axis_index(axis)
    right = [(j, (j + 1) % n) for j in range(n)]
    left = [(j, (j - 1) % n) for j in range(n)]
    bl = lax.dynamic_index_in_dim(xl, (i - 1) % n, 0, keepdims=False)
    br = lax.dynamic_index_in_dim(xr, (i + 1) % n, 0, keepdims=False)
    for s in range(n - 1):
        rl = lax.ppermute(bl, axis, right)
        rr = lax.ppermute(br, axis, left)
        bl = rl + lax.dynamic_index_in_dim(xl, (i - s - 2) % n, 0, keepdims=False)
        br = rr + lax.dynamic_index_in_dim(xr, (i + s + 2) % n, 0, keepdims=False)
    return bl, br


def ring_all_gather(x, axis, n):
    i = lax.axis_index(axis)
    h = x.shape[0] // 2
    right = [(j, (j + 1) % n) for j in range(n)]
    left = [(j, (j - 1) % n) for j in range(n)]
    out = jnp.zeros((n,) + x.shape, x.dtype)
    out = lax.dynamic_update_index_in_dim(out, x, i, 0)
    bl, br = x[:h], x[h:]
    zeros = (0,) * (x.ndim - 1)
    for s in range(n - 1):
        bl = lax.ppermute(bl, axis, right)
        br = lax.ppermute(br, axis, left)
        out = lax.dynamic_update_slice(out, bl[None], ((i - s - 1) % n, 0) + zeros)
        out = lax.dynamic_update_slice(out, br[None], ((i + s + 1) % n, h) + zeros)
    return out


def per_device(user_emb0, item_base, weight_tiles, blk_user, blk_item, blk_weight, *, sizes):
    n_ylo, n_x, n_z, n_yhi, n_core = sizes
    n_users = n_ylo * n_x * n_z
    tile_rows = weight_tiles.shape[1]
    width = user_emb0.shape[1]
    n_user_tiles = user_emb0.shape[0] // tile_rows
    user_tiles_t = jnp.swapaxes(user_emb0.astype(jnp.bfloat16).reshape(-1, tile_rows, width), 1, 2)
    users_list = blk_user.reshape(-1)
    items_list = blk_item.reshape(-1)
    weights_list = blk_weight.reshape(-1)

    item_ylo = items_list // (n_x * n_z)
    item_x = (items_list // n_z) % n_x
    item_z = items_list % n_z
    item_slot = (item_ylo * n_z + item_z) * n_x + item_x
    item_index = jnp.concatenate([users_list, weights_list, item_slot])
    partial_t = block_sums(item_index, user_tiles_t, weight_tiles, n_users)
    halves = partial_t.reshape(n_ylo, n_z, n_x * tile_rows, width)
    bl, br = ring_reduce_scatter_halves(halves[0], halves[1], "z", n_z)
    x = jnp.concatenate([bl, br], 0).reshape(n_ylo * n_x, tile_rows, width)
    x = lax.all_to_all(x, ("ylo", "x"), 0, 0, tiled=True)
    own_sum = x.sum(0).T

    position = lax.axis_index(USER_AXES)
    own_base = lax.dynamic_slice_in_dim(item_base[0], position * tile_rows, tile_rows, 0)
    own_emb = (1.0 - teleport) * own_sum + teleport * own_base
    own_bf_t = own_emb.astype(jnp.bfloat16).T
    t = lax.all_to_all(jnp.broadcast_to(own_bf_t[None], (n_z, width, tile_rows)), "z", 0, 0, tiled=True)
    t = jnp.broadcast_to(t[None], (n_ylo * n_x, n_z, width, tile_rows))
    t = lax.all_to_all(t, ("ylo", "x"), 0, 0, tiled=True)
    item_tiles_t = t.reshape(n_users, width, tile_rows)

    user_index = jnp.concatenate([weights_list, items_list, users_list])
    user_part = block_sums(user_index, weight_tiles, item_tiles_t, n_user_tiles, b_transposed=True)
    y = user_part.reshape(n_core, -1, width)
    y = ring_reduce_scatter(y, "core", n_core)
    y = ring_reduce_scatter(y.reshape(n_yhi, -1, width), "yhi", n_yhi)
    y = ring_all_gather(y, "yhi", n_yhi).reshape(-1, width)
    y = ring_all_gather(y, "core", n_core).reshape(-1, width)
    user_out = (1.0 - teleport) * y + teleport * user_emb0
    return (user_out, own_emb[None])


def solution(mesh):
    import functools

    sizes = (2, 4, 8, 2, 2)
    fine = Mesh(mesh.devices.reshape(sizes), USER_AXES + PANEL_AXES)
    placed = (
        P(USER_AXES, None),
        P(PANEL_AXES, None, None),
        P(),
        P(USER_AXES, PANEL_AXES, None),
        P(USER_AXES, PANEL_AXES, None),
        P(USER_AXES, PANEL_AXES, None),
    )
    return jax.shard_map(
        functools.partial(per_device, sizes=sizes),
        mesh=fine,
        in_specs=placed,
        out_specs=(P(USER_AXES, None), P(PANEL_AXES, USER_AXES, None)),
        check_vma=False,
    )
```

```python
import jax
import jax.numpy as jnp
from jax import lax
from jax.experimental import pallas as pl
from jax.experimental.pallas import tpu as pltpu
from jax.sharding import Mesh
from jax.sharding import PartitionSpec as P

teleport = 0.2

USER_AXES = ("ylo", "x", "z")
PANEL_AXES = ("yhi", "core")


def block_sum_kernel(index_ref, a_ref, b_ref, o_ref, *, b_transposed):
    o_ref[...] = jnp.zeros(o_ref.shape, o_ref.dtype)
    n_blocks = index_ref.shape[0] // 3

    def body(k, carry):
        a = a_ref[index_ref[k]]
        b = b_ref[index_ref[n_blocks + k]]
        contract = ((1,), (1,) if b_transposed else (0,))
        o_ref[index_ref[2 * n_blocks + k]] += lax.dot_general(
            a, b, (contract, ((), ())), preferred_element_type=jnp.float32
        )
        return carry

    lax.fori_loop(0, n_blocks, body, 0, unroll=32)


def block_sums(index, a_tiles, b_tiles, n_out, b_transposed=False):
    import functools

    tile = a_tiles.shape[1]
    width = b_tiles.shape[1] if b_transposed else b_tiles.shape[2]
    return pl.pallas_call(
        functools.partial(block_sum_kernel, b_transposed=b_transposed),
        grid_spec=pltpu.PrefetchScalarGridSpec(
            num_scalar_prefetch=1,
            grid=(1,),
            in_specs=[
                pl.BlockSpec(a_tiles.shape, lambda i, *_: (0, 0, 0)),
                pl.BlockSpec(b_tiles.shape, lambda i, *_: (0, 0, 0)),
            ],
            out_specs=pl.BlockSpec((n_out, tile, width), lambda i, *_: (0, 0, 0)),
        ),
        out_shape=jax.ShapeDtypeStruct((n_out, tile, width), jnp.float32),
    )(index, a_tiles, b_tiles)


def ring_reduce_scatter(x, axis, n):
    h = x.shape[1] // 2
    return jnp.concatenate(ring_reduce_scatter_halves(x[:, :h], x[:, h:], axis, n), 0)


def ring_reduce_scatter_halves(xl, xr, axis, n):
    i = lax.axis_index(axis)
    right = [(j, (j + 1) % n) for j in range(n)]
    left = [(j, (j - 1) % n) for j in range(n)]
    bl = lax.dynamic_index_in_dim(xl, (i - 1) % n, 0, keepdims=False)
    br = lax.dynamic_index_in_dim(xr, (i + 1) % n, 0, keepdims=False)
    for s in range(n - 1):
        rl = lax.ppermute(bl, axis, right)
        rr = lax.ppermute(br, axis, left)
        bl = rl + lax.dynamic_index_in_dim(xl, (i - s - 2) % n, 0, keepdims=False)
        br = rr + lax.dynamic_index_in_dim(xr, (i + s + 2) % n, 0, keepdims=False)
    return bl, br


def ring_all_gather(x, axis, n):
    i = lax.axis_index(axis)
    h = x.shape[0] // 2
    right = [(j, (j + 1) % n) for j in range(n)]
    left = [(j, (j - 1) % n) for j in range(n)]
    out = jnp.zeros((n,) + x.shape, x.dtype)
    out = lax.dynamic_update_index_in_dim(out, x, i, 0)
    bl, br = x[:h], x[h:]
    zeros = (0,) * (x.ndim - 1)
    for s in range(n - 1):
        bl = lax.ppermute(bl, axis, right)
        br = lax.ppermute(br, axis, left)
        out = lax.dynamic_update_slice(out, bl[None], ((i - s - 1) % n, 0) + zeros)
        out = lax.dynamic_update_slice(out, br[None], ((i + s + 1) % n, h) + zeros)
    return out


def per_device(user_emb0, item_base, weight_tiles, blk_user, blk_item, blk_weight, *, sizes):
    n_ylo, n_x, n_z, n_yhi, n_core = sizes
    n_users = n_ylo * n_x * n_z
    tile_rows = weight_tiles.shape[1]
    width = user_emb0.shape[1]
    n_user_tiles = user_emb0.shape[0] // tile_rows
    user_tiles_t = jnp.swapaxes(user_emb0.astype(jnp.bfloat16).reshape(-1, tile_rows, width), 1, 2)
    users_list = blk_user.reshape(-1)
    items_list = blk_item.reshape(-1)
    weights_list = blk_weight.reshape(-1)

    item_ylo = items_list // (n_x * n_z)
    item_x = (items_list // n_z) % n_x
    item_z = items_list % n_z
    item_slot = (item_ylo * n_z + item_z) * n_x + item_x
    item_index = jnp.concatenate([users_list, weights_list, item_slot])
    partial_t = block_sums(item_index, user_tiles_t, weight_tiles, n_users)
    halves = partial_t.reshape(n_ylo, n_z, n_x * tile_rows, width)
    bl, br = ring_reduce_scatter_halves(halves[0], halves[1], "z", n_z)
    x = jnp.concatenate([bl, br], 0).reshape(n_ylo * n_x, tile_rows, width)
    x = lax.all_to_all(x, ("ylo", "x"), 0, 0, tiled=True)
    own_sum = x.sum(0).T

    position = lax.axis_index(USER_AXES)
    own_base = lax.dynamic_slice_in_dim(item_base[0], position * tile_rows, tile_rows, 0)
    own_emb = (1.0 - teleport) * own_sum + teleport * own_base
    own_bf = own_emb.astype(jnp.bfloat16)
    t = lax.all_to_all(jnp.broadcast_to(own_bf[None], (n_z, tile_rows, width)), "z", 0, 0, tiled=True)
    t = jnp.broadcast_to(t[None], (n_ylo * n_x, n_z, tile_rows, width))
    t = lax.all_to_all(t, ("ylo", "x"), 0, 0, tiled=True)
    item_tiles = t.reshape(n_users, tile_rows, width)

    user_index = jnp.concatenate([weights_list, items_list, users_list])
    user_part = block_sums(user_index, weight_tiles, item_tiles, n_user_tiles)
    y = user_part.reshape(n_core, -1, width)
    y = ring_reduce_scatter(y, "core", n_core)
    y = ring_reduce_scatter(y.reshape(n_yhi, -1, width), "yhi", n_yhi)
    y = ring_all_gather(y, "yhi", n_yhi).reshape(-1, width)
    y = ring_all_gather(y, "core", n_core).reshape(-1, width)
    user_out = (1.0 - teleport) * y + teleport * user_emb0
    return (user_out, own_emb[None])


def solution(mesh):
    import functools

    sizes = (2, 4, 8, 2, 2)
    fine = Mesh(mesh.devices.reshape(sizes), USER_AXES + PANEL_AXES)
    placed = (
        P(USER_AXES, None),
        P(PANEL_AXES, None, None),
        P(),
        P(USER_AXES, PANEL_AXES, None),
        P(USER_AXES, PANEL_AXES, None),
        P(USER_AXES, PANEL_AXES, None),
    )
    return jax.shard_map(
        functools.partial(per_device, sizes=sizes),
        mesh=fine,
        in_specs=placed,
        out_specs=(P(USER_AXES, None), P(PANEL_AXES, USER_AXES, None)),
        check_vma=False,
    )
```

```python
import jax
import jax.numpy as jnp
from jax import lax
from jax.experimental import pallas as pl
from jax.experimental.pallas import tpu as pltpu
from jax.sharding import Mesh
from jax.sharding import PartitionSpec as P

teleport = 0.2

USER_AXES = ("ylo", "x", "z")
PANEL_AXES = ("yhi", "core")


def block_sum_kernel(index_ref, a_ref, b_ref, o_ref, *, b_transposed):
    o_ref[...] = jnp.zeros(o_ref.shape, o_ref.dtype)
    n_blocks = index_ref.shape[0] // 3

    def body(k, carry):
        a = a_ref[index_ref[k]]
        b = b_ref[index_ref[n_blocks + k]]
        contract = ((1,), (1,) if b_transposed else (0,))
        o_ref[index_ref[2 * n_blocks + k]] += lax.dot_general(
            a, b, (contract, ((), ())), preferred_element_type=jnp.float32
        )
        return carry

    lax.fori_loop(0, n_blocks, body, 0, unroll=32)


def block_sums(index, a_tiles, b_tiles, n_out, b_transposed=False):
    import functools

    tile = a_tiles.shape[1]
    width = b_tiles.shape[1] if b_transposed else b_tiles.shape[2]
    return pl.pallas_call(
        functools.partial(block_sum_kernel, b_transposed=b_transposed),
        grid_spec=pltpu.PrefetchScalarGridSpec(
            num_scalar_prefetch=1,
            grid=(1,),
            in_specs=[
                pl.BlockSpec(a_tiles.shape, lambda i, *_: (0, 0, 0)),
                pl.BlockSpec(b_tiles.shape, lambda i, *_: (0, 0, 0)),
            ],
            out_specs=pl.BlockSpec((n_out, tile, width), lambda i, *_: (0, 0, 0)),
        ),
        out_shape=jax.ShapeDtypeStruct((n_out, tile, width), jnp.float32),
    )(index, a_tiles, b_tiles)


def ring_reduce_scatter(x, axis, n):
    h = x.shape[1] // 2
    return jnp.concatenate(ring_reduce_scatter_halves(x[:, :h], x[:, h:], axis, n), 0)


def ring_reduce_scatter_halves(xl, xr, axis, n):
    i = lax.axis_index(axis)
    if xr is None:
        both = xl

        def chunk(side, j):
            return both[side, j]

    else:

        def chunk(side, j):
            return lax.dynamic_index_in_dim((xl, xr)[side], j, 0, keepdims=False)

    right = [(j, (j + 1) % n) for j in range(n)]
    left = [(j, (j - 1) % n) for j in range(n)]
    bl = chunk(0, (i - 1) % n)
    br = chunk(1, (i + 1) % n)
    for s in range(n - 1):
        rl = lax.ppermute(bl, axis, right)
        rr = lax.ppermute(br, axis, left)
        bl = rl + chunk(0, (i - s - 2) % n)
        br = rr + chunk(1, (i + s + 2) % n)
    return bl, br


def ring_all_gather(x, axis, n):
    i = lax.axis_index(axis)
    h = x.shape[0] // 2
    right = [(j, (j + 1) % n) for j in range(n)]
    left = [(j, (j - 1) % n) for j in range(n)]
    out = jnp.zeros((n,) + x.shape, x.dtype)
    out = lax.dynamic_update_index_in_dim(out, x, i, 0)
    bl, br = x[:h], x[h:]
    zeros = (0,) * (x.ndim - 1)
    for s in range(n - 1):
        bl = lax.ppermute(bl, axis, right)
        br = lax.ppermute(br, axis, left)
        out = lax.dynamic_update_slice(out, bl[None], ((i - s - 1) % n, 0) + zeros)
        out = lax.dynamic_update_slice(out, br[None], ((i + s + 1) % n, h) + zeros)
    return out


def per_device(user_emb0, item_base, weight_tiles, blk_user, blk_item, blk_weight, *, sizes):
    n_ylo, n_x, n_z, n_yhi, n_core = sizes
    n_users = n_ylo * n_x * n_z
    tile_rows = weight_tiles.shape[1]
    width = user_emb0.shape[1]
    n_user_tiles = user_emb0.shape[0] // tile_rows
    user_tiles_t = jnp.swapaxes(user_emb0.astype(jnp.bfloat16).reshape(-1, tile_rows, width), 1, 2)
    users_list = blk_user.reshape(-1)
    items_list = blk_item.reshape(-1)
    weights_list = blk_weight.reshape(-1)

    item_ylo = items_list // (n_x * n_z)
    item_x = (items_list // n_z) % n_x
    item_z = items_list % n_z
    item_slot = (item_ylo * n_z + item_z) * n_x + item_x
    item_index = jnp.concatenate([users_list, weights_list, item_slot])
    partial_t = block_sums(item_index, user_tiles_t, weight_tiles, n_users)
    halves = partial_t.reshape(n_ylo, n_z, n_x * tile_rows, width)
    bl, br = ring_reduce_scatter_halves(halves, None, "z", n_z)
    x = jnp.concatenate([bl, br], 0).reshape(n_ylo * n_x, tile_rows, width)
    x = lax.all_to_all(x, ("ylo", "x"), 0, 0, tiled=True)
    own_sum = x.sum(0).T

    position = lax.axis_index(USER_AXES)
    own_base = lax.dynamic_slice_in_dim(item_base[0], position * tile_rows, tile_rows, 0)
    own_emb = (1.0 - teleport) * own_sum + teleport * own_base
    own_bf = own_emb.astype(jnp.bfloat16)
    t = lax.all_to_all(jnp.broadcast_to(own_bf[None], (n_z, tile_rows, width)), "z", 0, 0, tiled=True)
    t = jnp.broadcast_to(t[None], (n_ylo * n_x, n_z, tile_rows, width))
    t = lax.all_to_all(t, ("ylo", "x"), 0, 0, tiled=True)
    item_tiles = t.reshape(n_users, tile_rows, width)

    user_index = jnp.concatenate([weights_list, items_list, users_list])
    user_part = block_sums(user_index, weight_tiles, item_tiles, n_user_tiles)
    y = user_part.reshape(n_core, -1, width)
    y = ring_reduce_scatter(y, "core", n_core)
    y = ring_reduce_scatter(y.reshape(n_yhi, -1, width), "yhi", n_yhi)
    y = ring_all_gather(y, "yhi", n_yhi).reshape(-1, width)
    y = ring_all_gather(y, "core", n_core).reshape(-1, width)
    user_out = (1.0 - teleport) * y + teleport * user_emb0
    return (user_out, own_emb[None])


def solution(mesh):
    import functools

    sizes = (2, 4, 8, 2, 2)
    fine = Mesh(mesh.devices.reshape(sizes), USER_AXES + PANEL_AXES)
    placed = (
        P(USER_AXES, None),
        P(PANEL_AXES, None, None),
        P(),
        P(USER_AXES, PANEL_AXES, None),
        P(USER_AXES, PANEL_AXES, None),
        P(USER_AXES, PANEL_AXES, None),
    )
    return jax.shard_map(
        functools.partial(per_device, sizes=sizes),
        mesh=fine,
        in_specs=placed,
        out_specs=(P(USER_AXES, None), P(PANEL_AXES, USER_AXES, None)),
        check_vma=False,
    )
```

```python
import jax
import jax.numpy as jnp
from jax import lax
from jax.experimental import pallas as pl
from jax.experimental.pallas import tpu as pltpu
from jax.sharding import Mesh
from jax.sharding import PartitionSpec as P

teleport = 0.2

USER_AXES = ("ylo", "x", "z")
PANEL_AXES = ("yhi", "core")


def block_sum_kernel(index_ref, a_ref, b_ref, o_ref, *, b_transposed):
    o_ref[...] = jnp.zeros(o_ref.shape, o_ref.dtype)
    n_blocks = index_ref.shape[0] // 3

    def body(k, carry):
        a = a_ref[index_ref[k]]
        b = b_ref[index_ref[n_blocks + k]]
        contract = ((1,), (1,) if b_transposed else (0,))
        o_ref[index_ref[2 * n_blocks + k]] += lax.dot_general(
            a, b, (contract, ((), ())), preferred_element_type=jnp.float32
        )
        return carry

    lax.fori_loop(0, n_blocks, body, 0, unroll=32)


def block_sums(index, a_tiles, b_tiles, n_out, b_transposed=False):
    import functools

    tile = a_tiles.shape[1]
    width = b_tiles.shape[1] if b_transposed else b_tiles.shape[2]
    return pl.pallas_call(
        functools.partial(block_sum_kernel, b_transposed=b_transposed),
        grid_spec=pltpu.PrefetchScalarGridSpec(
            num_scalar_prefetch=1,
            grid=(1,),
            in_specs=[
                pl.BlockSpec(a_tiles.shape, lambda i, *_: (0, 0, 0)),
                pl.BlockSpec(b_tiles.shape, lambda i, *_: (0, 0, 0)),
            ],
            out_specs=pl.BlockSpec((n_out, tile, width), lambda i, *_: (0, 0, 0)),
        ),
        out_shape=jax.ShapeDtypeStruct((n_out, tile, width), jnp.float32),
    )(index, a_tiles, b_tiles)


def ring_reduce_scatter(x, axis, n):
    h = x.shape[1] // 2
    return jnp.concatenate(ring_reduce_scatter_halves(x[:, :h], x[:, h:], axis, n), 0)


def ring_reduce_scatter_halves(xl, xr, axis, n):
    i = lax.axis_index(axis)
    right = [(j, (j + 1) % n) for j in range(n)]
    left = [(j, (j - 1) % n) for j in range(n)]
    bl = lax.dynamic_index_in_dim(xl, (i - 1) % n, 0, keepdims=False)
    br = lax.dynamic_index_in_dim(xr, (i + 1) % n, 0, keepdims=False)
    for s in range(n - 1):
        rl = lax.ppermute(bl, axis, right)
        rr = lax.ppermute(br, axis, left)
        bl = rl + lax.dynamic_index_in_dim(xl, (i - s - 2) % n, 0, keepdims=False)
        br = rr + lax.dynamic_index_in_dim(xr, (i + s + 2) % n, 0, keepdims=False)
    return bl, br


def ring_all_gather(x, axis, n):
    i = lax.axis_index(axis)
    h = x.shape[0] // 2
    right = [(j, (j + 1) % n) for j in range(n)]
    left = [(j, (j - 1) % n) for j in range(n)]
    out = jnp.zeros((n,) + x.shape, x.dtype)
    out = lax.dynamic_update_index_in_dim(out, x, i, 0)
    bl, br = x[:h], x[h:]
    zeros = (0,) * (x.ndim - 1)
    for s in range(n - 1):
        bl = lax.ppermute(bl, axis, right)
        br = lax.ppermute(br, axis, left)
        out = lax.dynamic_update_slice(out, bl[None], ((i - s - 1) % n, 0) + zeros)
        out = lax.dynamic_update_slice(out, br[None], ((i + s + 1) % n, h) + zeros)
    return out


def per_device(user_emb0, item_base, weight_tiles, blk_user, blk_item, blk_weight, *, sizes):
    n_ylo, n_x, n_z, n_yhi, n_core = sizes
    n_users = n_ylo * n_x * n_z
    tile_rows = weight_tiles.shape[1]
    width = user_emb0.shape[1]
    n_user_tiles = user_emb0.shape[0] // tile_rows
    user_tiles_t = jnp.swapaxes(user_emb0.astype(jnp.bfloat16).reshape(-1, tile_rows, width), 1, 2)
    users_list = blk_user.reshape(-1)
    items_list = blk_item.reshape(-1)
    weights_list = blk_weight.reshape(-1)

    item_ylo = items_list // (n_x * n_z)
    item_x = (items_list // n_z) % n_x
    item_z = items_list % n_z
    item_slot = (item_ylo * n_z + item_z) * n_x + item_x
    item_index = jnp.concatenate([users_list, weights_list, item_slot])
    partial_t = block_sums(item_index, user_tiles_t, weight_tiles, n_users)
    halves = partial_t.reshape(n_ylo, n_z, n_x * tile_rows, width)
    bl, br = ring_reduce_scatter_halves(halves[0], halves[1], "z", n_z)
    x = jnp.concatenate([bl, br], 0).reshape(n_ylo * n_x, tile_rows, width)
    x = lax.all_to_all(x, ("ylo", "x"), 0, 0, tiled=True)
    own_sum = x.sum(0).T

    position = lax.axis_index(USER_AXES)
    own_base = lax.dynamic_slice_in_dim(item_base[0], position * tile_rows, tile_rows, 0)
    own_emb = (1.0 - teleport) * own_sum + teleport * own_base
    own_bf = own_emb.astype(jnp.bfloat16)
    t = lax.all_to_all(
        jnp.broadcast_to(own_bf[None], (n_ylo * n_x, tile_rows, width)), ("ylo", "x"), 0, 0, tiled=True
    )
    t = jnp.broadcast_to(t[None], (n_z, n_ylo * n_x, tile_rows, width))
    t = lax.all_to_all(t, "z", 0, 0, tiled=True)
    item_tiles = t.reshape(n_users, tile_rows, width)
    gathered_slot = (item_z * n_ylo + item_ylo) * n_x + item_x

    user_index = jnp.concatenate([weights_list, gathered_slot, users_list])
    user_part = block_sums(user_index, weight_tiles, item_tiles, n_user_tiles)
    y = user_part.reshape(n_core, -1, width)
    y = ring_reduce_scatter(y, "core", n_core)
    y = ring_reduce_scatter(y.reshape(n_yhi, -1, width), "yhi", n_yhi)
    y = ring_all_gather(y, "yhi", n_yhi).reshape(-1, width)
    y = ring_all_gather(y, "core", n_core).reshape(-1, width)
    user_out = (1.0 - teleport) * y + teleport * user_emb0
    return (user_out, own_emb[None])


def solution(mesh):
    import functools

    sizes = (2, 4, 8, 2, 2)
    fine = Mesh(mesh.devices.reshape(sizes), USER_AXES + PANEL_AXES)
    placed = (
        P(USER_AXES, None),
        P(PANEL_AXES, None, None),
        P(),
        P(USER_AXES, PANEL_AXES, None),
        P(USER_AXES, PANEL_AXES, None),
        P(USER_AXES, PANEL_AXES, None),
    )
    return jax.shard_map(
        functools.partial(per_device, sizes=sizes),
        mesh=fine,
        in_specs=placed,
        out_specs=(P(USER_AXES, None), P(PANEL_AXES, USER_AXES, None)),
        check_vma=False,
    )
```

```python
import jax
import jax.numpy as jnp
from jax import lax
from jax.experimental import pallas as pl
from jax.experimental.pallas import tpu as pltpu
from jax.sharding import Mesh
from jax.sharding import PartitionSpec as P

teleport = 0.2

USER_AXES = ("ylo", "x", "z")
PANEL_AXES = ("yhi", "core")


def block_sum_kernel(index_ref, a_ref, b_ref, o_ref, *, b_transposed):
    o_ref[...] = jnp.zeros(o_ref.shape, o_ref.dtype)
    n_blocks = index_ref.shape[0] // 3

    def body(k, carry):
        a = a_ref[index_ref[k]]
        b = b_ref[index_ref[n_blocks + k]]
        contract = ((1,), (1,) if b_transposed else (0,))
        o_ref[index_ref[2 * n_blocks + k]] += lax.dot_general(
            a, b, (contract, ((), ())), preferred_element_type=jnp.float32
        )
        return carry

    lax.fori_loop(0, n_blocks, body, 0, unroll=64)


def block_sums(index, a_tiles, b_tiles, n_out, b_transposed=False):
    import functools

    tile = a_tiles.shape[1]
    width = b_tiles.shape[1] if b_transposed else b_tiles.shape[2]
    return pl.pallas_call(
        functools.partial(block_sum_kernel, b_transposed=b_transposed),
        grid_spec=pltpu.PrefetchScalarGridSpec(
            num_scalar_prefetch=1,
            grid=(1,),
            in_specs=[
                pl.BlockSpec(a_tiles.shape, lambda i, *_: (0, 0, 0)),
                pl.BlockSpec(b_tiles.shape, lambda i, *_: (0, 0, 0)),
            ],
            out_specs=pl.BlockSpec((n_out, tile, width), lambda i, *_: (0, 0, 0)),
        ),
        out_shape=jax.ShapeDtypeStruct((n_out, tile, width), jnp.float32),
    )(index, a_tiles, b_tiles)


def ring_reduce_scatter(x, axis, n):
    h = x.shape[1] // 2
    return jnp.concatenate(ring_reduce_scatter_halves(x[:, :h], x[:, h:], axis, n), 0)


def ring_reduce_scatter_halves(xl, xr, axis, n):
    i = lax.axis_index(axis)
    right = [(j, (j + 1) % n) for j in range(n)]
    left = [(j, (j - 1) % n) for j in range(n)]
    bl = lax.dynamic_index_in_dim(xl, (i - 1) % n, 0, keepdims=False)
    br = lax.dynamic_index_in_dim(xr, (i + 1) % n, 0, keepdims=False)
    for s in range(n - 1):
        rl = lax.ppermute(bl, axis, right)
        rr = lax.ppermute(br, axis, left)
        bl = rl + lax.dynamic_index_in_dim(xl, (i - s - 2) % n, 0, keepdims=False)
        br = rr + lax.dynamic_index_in_dim(xr, (i + s + 2) % n, 0, keepdims=False)
    return bl, br


def ring_all_gather(x, axis, n):
    i = lax.axis_index(axis)
    h = x.shape[0] // 2
    right = [(j, (j + 1) % n) for j in range(n)]
    left = [(j, (j - 1) % n) for j in range(n)]
    out = jnp.zeros((n,) + x.shape, x.dtype)
    out = lax.dynamic_update_index_in_dim(out, x, i, 0)
    bl, br = x[:h], x[h:]
    zeros = (0,) * (x.ndim - 1)
    for s in range(n - 1):
        bl = lax.ppermute(bl, axis, right)
        br = lax.ppermute(br, axis, left)
        out = lax.dynamic_update_slice(out, bl[None], ((i - s - 1) % n, 0) + zeros)
        out = lax.dynamic_update_slice(out, br[None], ((i + s + 1) % n, h) + zeros)
    return out


def per_device(user_emb0, item_base, weight_tiles, blk_user, blk_item, blk_weight, *, sizes):
    n_ylo, n_x, n_z, n_yhi, n_core = sizes
    n_users = n_ylo * n_x * n_z
    tile_rows = weight_tiles.shape[1]
    width = user_emb0.shape[1]
    n_user_tiles = user_emb0.shape[0] // tile_rows
    user_tiles_t = jnp.swapaxes(user_emb0.astype(jnp.bfloat16).reshape(-1, tile_rows, width), 1, 2)
    users_list = blk_user.reshape(-1)
    items_list = blk_item.reshape(-1)
    weights_list = blk_weight.reshape(-1)

    item_ylo = items_list // (n_x * n_z)
    item_x = (items_list // n_z) % n_x
    item_z = items_list % n_z
    item_slot = (item_ylo * n_z + item_z) * n_x + item_x
    item_index = jnp.concatenate([users_list, weights_list, item_slot])
    partial_t = block_sums(item_index, user_tiles_t, weight_tiles, n_users)
    halves = partial_t.reshape(n_ylo, n_z, n_x * tile_rows, width)
    bl, br = ring_reduce_scatter_halves(halves[0], halves[1], "z", n_z)
    x = jnp.concatenate([bl, br], 0).reshape(n_ylo * n_x, tile_rows, width)
    x = lax.all_to_all(x, ("ylo", "x"), 0, 0, tiled=True)
    own_sum = x.sum(0).T

    position = lax.axis_index(USER_AXES)
    own_base = lax.dynamic_slice_in_dim(item_base[0], position * tile_rows, tile_rows, 0)
    own_emb = (1.0 - teleport) * own_sum + teleport * own_base
    own_bf = own_emb.astype(jnp.bfloat16)
    t = lax.all_to_all(jnp.broadcast_to(own_bf[None], (n_z, tile_rows, width)), "z", 0, 0, tiled=True)
    t = jnp.broadcast_to(t[None], (n_ylo * n_x, n_z, tile_rows, width))
    t = lax.all_to_all(t, ("ylo", "x"), 0, 0, tiled=True)
    item_tiles = t.reshape(n_users, tile_rows, width)

    user_index = jnp.concatenate([weights_list, items_list, users_list])
    user_part = block_sums(user_index, weight_tiles, item_tiles, n_user_tiles)
    y = user_part.reshape(n_core, -1, width)
    y = ring_reduce_scatter(y, "core", n_core)
    y = ring_reduce_scatter(y.reshape(n_yhi, -1, width), "yhi", n_yhi)
    y = ring_all_gather(y, "yhi", n_yhi).reshape(-1, width)
    y = ring_all_gather(y, "core", n_core).reshape(-1, width)
    user_out = (1.0 - teleport) * y + teleport * user_emb0
    return (user_out, own_emb[None])


def solution(mesh):
    import functools

    sizes = (2, 4, 8, 2, 2)
    fine = Mesh(mesh.devices.reshape(sizes), USER_AXES + PANEL_AXES)
    placed = (
        P(USER_AXES, None),
        P(PANEL_AXES, None, None),
        P(),
        P(USER_AXES, PANEL_AXES, None),
        P(USER_AXES, PANEL_AXES, None),
        P(USER_AXES, PANEL_AXES, None),
    )
    return jax.shard_map(
        functools.partial(per_device, sizes=sizes),
        mesh=fine,
        in_specs=placed,
        out_specs=(P(USER_AXES, None), P(PANEL_AXES, USER_AXES, None)),
        check_vma=False,
    )
```

```python
import jax
import jax.numpy as jnp
from jax import lax
from jax.experimental import pallas as pl
from jax.experimental.pallas import tpu as pltpu
from jax.sharding import Mesh
from jax.sharding import PartitionSpec as P

teleport = 0.2

USER_AXES = ("ylo", "x", "z")
PANEL_AXES = ("yhi", "core")


def block_sum_kernel(index_ref, a_ref, b_ref, o_ref, *, b_transposed):
    o_ref[...] = jnp.zeros(o_ref.shape, o_ref.dtype)
    n_blocks = index_ref.shape[0] // 3

    def body(k, carry):
        a = a_ref[index_ref[k]]
        b = b_ref[index_ref[n_blocks + k]]
        contract = ((1,), (1,) if b_transposed else (0,))
        o_ref[index_ref[2 * n_blocks + k]] += lax.dot_general(
            a, b, (contract, ((), ())), preferred_element_type=jnp.float32
        )
        return carry

    lax.fori_loop(0, n_blocks, body, 0, unroll=128)


def block_sums(index, a_tiles, b_tiles, n_out, b_transposed=False):
    import functools

    tile = a_tiles.shape[1]
    width = b_tiles.shape[1] if b_transposed else b_tiles.shape[2]
    return pl.pallas_call(
        functools.partial(block_sum_kernel, b_transposed=b_transposed),
        grid_spec=pltpu.PrefetchScalarGridSpec(
            num_scalar_prefetch=1,
            grid=(1,),
            in_specs=[
                pl.BlockSpec(a_tiles.shape, lambda i, *_: (0, 0, 0)),
                pl.BlockSpec(b_tiles.shape, lambda i, *_: (0, 0, 0)),
            ],
            out_specs=pl.BlockSpec((n_out, tile, width), lambda i, *_: (0, 0, 0)),
        ),
        out_shape=jax.ShapeDtypeStruct((n_out, tile, width), jnp.float32),
    )(index, a_tiles, b_tiles)


def ring_reduce_scatter(x, axis, n):
    h = x.shape[1] // 2
    return jnp.concatenate(ring_reduce_scatter_halves(x[:, :h], x[:, h:], axis, n), 0)


def ring_reduce_scatter_halves(xl, xr, axis, n):
    i = lax.axis_index(axis)
    right = [(j, (j + 1) % n) for j in range(n)]
    left = [(j, (j - 1) % n) for j in range(n)]
    bl = lax.dynamic_index_in_dim(xl, (i - 1) % n, 0, keepdims=False)
    br = lax.dynamic_index_in_dim(xr, (i + 1) % n, 0, keepdims=False)
    for s in range(n - 1):
        rl = lax.ppermute(bl, axis, right)
        rr = lax.ppermute(br, axis, left)
        bl = rl + lax.dynamic_index_in_dim(xl, (i - s - 2) % n, 0, keepdims=False)
        br = rr + lax.dynamic_index_in_dim(xr, (i + s + 2) % n, 0, keepdims=False)
    return bl, br


def ring_all_gather(x, axis, n):
    i = lax.axis_index(axis)
    h = x.shape[0] // 2
    right = [(j, (j + 1) % n) for j in range(n)]
    left = [(j, (j - 1) % n) for j in range(n)]
    out = jnp.zeros((n,) + x.shape, x.dtype)
    out = lax.dynamic_update_index_in_dim(out, x, i, 0)
    bl, br = x[:h], x[h:]
    zeros = (0,) * (x.ndim - 1)
    for s in range(n - 1):
        bl = lax.ppermute(bl, axis, right)
        br = lax.ppermute(br, axis, left)
        out = lax.dynamic_update_slice(out, bl[None], ((i - s - 1) % n, 0) + zeros)
        out = lax.dynamic_update_slice(out, br[None], ((i + s + 1) % n, h) + zeros)
    return out


def per_device(user_emb0, item_base, weight_tiles, blk_user, blk_item, blk_weight, *, sizes):
    n_ylo, n_x, n_z, n_yhi, n_core = sizes
    n_users = n_ylo * n_x * n_z
    tile_rows = weight_tiles.shape[1]
    width = user_emb0.shape[1]
    n_user_tiles = user_emb0.shape[0] // tile_rows
    user_tiles_t = jnp.swapaxes(user_emb0.astype(jnp.bfloat16).reshape(-1, tile_rows, width), 1, 2)
    users_list = blk_user.reshape(-1)
    items_list = blk_item.reshape(-1)
    weights_list = blk_weight.reshape(-1)

    item_ylo = items_list // (n_x * n_z)
    item_x = (items_list // n_z) % n_x
    item_z = items_list % n_z
    item_slot = (item_ylo * n_z + item_z) * n_x + item_x
    item_index = jnp.concatenate([users_list, weights_list, item_slot])
    partial_t = block_sums(item_index, user_tiles_t, weight_tiles, n_users)
    halves = partial_t.reshape(n_ylo, n_z, n_x * tile_rows, width)
    bl, br = ring_reduce_scatter_halves(halves[0], halves[1], "z", n_z)
    x = jnp.concatenate([bl, br], 0).reshape(n_ylo * n_x, tile_rows, width)
    x = lax.all_to_all(x, ("ylo", "x"), 0, 0, tiled=True)
    own_sum = x.sum(0).T

    position = lax.axis_index(USER_AXES)
    own_base = lax.dynamic_slice_in_dim(item_base[0], position * tile_rows, tile_rows, 0)
    own_emb = (1.0 - teleport) * own_sum + teleport * own_base
    own_bf = own_emb.astype(jnp.bfloat16)
    t = lax.all_to_all(jnp.broadcast_to(own_bf[None], (n_z, tile_rows, width)), "z", 0, 0, tiled=True)
    t = jnp.broadcast_to(t[None], (n_ylo * n_x, n_z, tile_rows, width))
    t = lax.all_to_all(t, ("ylo", "x"), 0, 0, tiled=True)
    item_tiles = t.reshape(n_users, tile_rows, width)

    user_index = jnp.concatenate([weights_list, items_list, users_list])
    user_part = block_sums(user_index, weight_tiles, item_tiles, n_user_tiles)
    y = user_part.reshape(n_core, -1, width)
    y = ring_reduce_scatter(y, "core", n_core)
    y = ring_reduce_scatter(y.reshape(n_yhi, -1, width), "yhi", n_yhi)
    y = ring_all_gather(y, "yhi", n_yhi).reshape(-1, width)
    y = ring_all_gather(y, "core", n_core).reshape(-1, width)
    user_out = (1.0 - teleport) * y + teleport * user_emb0
    return (user_out, own_emb[None])


def solution(mesh):
    import functools

    sizes = (2, 4, 8, 2, 2)
    fine = Mesh(mesh.devices.reshape(sizes), USER_AXES + PANEL_AXES)
    placed = (
        P(USER_AXES, None),
        P(PANEL_AXES, None, None),
        P(),
        P(USER_AXES, PANEL_AXES, None),
        P(USER_AXES, PANEL_AXES, None),
        P(USER_AXES, PANEL_AXES, None),
    )
    return jax.shard_map(
        functools.partial(per_device, sizes=sizes),
        mesh=fine,
        in_specs=placed,
        out_specs=(P(USER_AXES, None), P(PANEL_AXES, USER_AXES, None)),
        check_vma=False,
    )
```

```python
import jax
import jax.numpy as jnp
from jax import lax
from jax.experimental import pallas as pl
from jax.experimental.pallas import tpu as pltpu
from jax.sharding import Mesh
from jax.sharding import PartitionSpec as P

teleport = 0.2

USER_AXES = ("ylo", "x", "z")
PANEL_AXES = ("yhi", "core")


def block_sum_kernel(index_ref, a_ref, b_ref, o_ref, *, b_transposed):
    o_ref[...] = jnp.zeros(o_ref.shape, o_ref.dtype)
    n_blocks = index_ref.shape[0] // 3

    def body(k, carry):
        a = a_ref[index_ref[k]]
        b = b_ref[index_ref[n_blocks + k]]
        contract = ((1,), (1,) if b_transposed else (0,))
        o_ref[index_ref[2 * n_blocks + k]] += lax.dot_general(
            a, b, (contract, ((), ())), preferred_element_type=jnp.float32
        )
        return carry

    lax.fori_loop(0, n_blocks, body, 0, unroll=64)


def block_sums(index, a_tiles, b_tiles, n_out, b_transposed=False):
    import functools

    tile = a_tiles.shape[1]
    width = b_tiles.shape[1] if b_transposed else b_tiles.shape[2]
    return pl.pallas_call(
        functools.partial(block_sum_kernel, b_transposed=b_transposed),
        grid_spec=pltpu.PrefetchScalarGridSpec(
            num_scalar_prefetch=1,
            grid=(1,),
            in_specs=[
                pl.BlockSpec(a_tiles.shape, lambda i, *_: (0, 0, 0)),
                pl.BlockSpec(b_tiles.shape, lambda i, *_: (0, 0, 0)),
            ],
            out_specs=pl.BlockSpec((n_out, tile, width), lambda i, *_: (0, 0, 0)),
        ),
        out_shape=jax.ShapeDtypeStruct((n_out, tile, width), jnp.float32),
    )(index, a_tiles, b_tiles)


def ring_reduce_scatter(x, axis, n):
    h = x.shape[1] // 2
    return jnp.concatenate(ring_reduce_scatter_halves(x[:, :h], x[:, h:], axis, n), 0)


def ring_reduce_scatter_halves(xl, xr, axis, n):
    i = lax.axis_index(axis)
    right = [(j, (j + 1) % n) for j in range(n)]
    left = [(j, (j - 1) % n) for j in range(n)]
    bl = lax.dynamic_index_in_dim(xl, (i - 1) % n, 0, keepdims=False)
    br = lax.dynamic_index_in_dim(xr, (i + 1) % n, 0, keepdims=False)
    for s in range(n - 1):
        rl = lax.ppermute(bl, axis, right)
        rr = lax.ppermute(br, axis, left)
        bl = rl + lax.dynamic_index_in_dim(xl, (i - s - 2) % n, 0, keepdims=False)
        br = rr + lax.dynamic_index_in_dim(xr, (i + s + 2) % n, 0, keepdims=False)
    return bl, br


def ring_all_gather(x, axis, n):
    i = lax.axis_index(axis)
    h = x.shape[0] // 2
    right = [(j, (j + 1) % n) for j in range(n)]
    left = [(j, (j - 1) % n) for j in range(n)]
    out = jnp.zeros((n,) + x.shape, x.dtype)
    out = lax.dynamic_update_index_in_dim(out, x, i, 0)
    bl, br = x[:h], x[h:]
    zeros = (0,) * (x.ndim - 1)
    for s in range(n - 1):
        bl = lax.ppermute(bl, axis, right)
        br = lax.ppermute(br, axis, left)
        out = lax.dynamic_update_slice(out, bl[None], ((i - s - 1) % n, 0) + zeros)
        out = lax.dynamic_update_slice(out, br[None], ((i + s + 1) % n, h) + zeros)
    return out


def per_device(user_emb0, item_base, weight_tiles, blk_user, blk_item, blk_weight, *, sizes):
    n_ylo, n_x, n_z, n_yhi, n_core = sizes
    n_users = n_ylo * n_x * n_z
    tile_rows = weight_tiles.shape[1]
    width = user_emb0.shape[1]
    n_user_tiles = user_emb0.shape[0] // tile_rows
    user_tiles_t = jnp.swapaxes(user_emb0.astype(jnp.bfloat16).reshape(-1, tile_rows, width), 1, 2)
    users_list = blk_user.reshape(-1)
    items_list = blk_item.reshape(-1)
    weights_list = blk_weight.reshape(-1)

    item_ylo = items_list // (n_x * n_z)
    item_x = (items_list // n_z) % n_x
    item_z = items_list % n_z
    item_slot = (item_ylo * n_z + item_z) * n_x + item_x
    item_index = jnp.concatenate([users_list, weights_list, item_slot])
    partial_t = block_sums(item_index, user_tiles_t, weight_tiles, n_users)
    halves = partial_t.reshape(n_ylo, n_z, n_x * tile_rows, width)
    bl, br = ring_reduce_scatter_halves(halves[0], halves[1], "z", n_z)
    x = jnp.concatenate([bl, br], 0).reshape(n_ylo * n_x, tile_rows, width)
    x = lax.all_to_all(x, ("ylo", "x"), 0, 0, tiled=True)
    own_sum = x.sum(0).T

    position = lax.axis_index(USER_AXES)
    own_base = lax.dynamic_slice_in_dim(item_base[0], position * tile_rows, tile_rows, 0)
    own_emb = (1.0 - teleport) * own_sum + teleport * own_base
    own_bf = own_emb.astype(jnp.bfloat16)
    t = lax.all_to_all(jnp.broadcast_to(own_bf[None], (n_z, tile_rows, width)), "z", 0, 0, tiled=True)
    t = jnp.broadcast_to(t[None], (n_ylo * n_x, n_z, tile_rows, width))
    t = lax.all_to_all(t, ("ylo", "x"), 0, 0, tiled=True)
    item_tiles = t.reshape(n_users, tile_rows, width)

    user_index = jnp.concatenate([weights_list, items_list, users_list])
    user_part = block_sums(user_index, weight_tiles, item_tiles, n_user_tiles)
    y = user_part.reshape(n_core, -1, width)
    y = ring_reduce_scatter(y, "core", n_core)
    y = y + lax.ppermute(y, "yhi", [(j, (j + 1) % n_yhi) for j in range(n_yhi)])
    y = ring_all_gather(y, "core", n_core).reshape(-1, width)
    user_out = (1.0 - teleport) * y + teleport * user_emb0
    return (user_out, own_emb[None])


def solution(mesh):
    import functools

    sizes = (2, 4, 8, 2, 2)
    fine = Mesh(mesh.devices.reshape(sizes), USER_AXES + PANEL_AXES)
    placed = (
        P(USER_AXES, None),
        P(PANEL_AXES, None, None),
        P(),
        P(USER_AXES, PANEL_AXES, None),
        P(USER_AXES, PANEL_AXES, None),
        P(USER_AXES, PANEL_AXES, None),
    )
    return jax.shard_map(
        functools.partial(per_device, sizes=sizes),
        mesh=fine,
        in_specs=placed,
        out_specs=(P(USER_AXES, None), P(PANEL_AXES, USER_AXES, None)),
        check_vma=False,
    )
```

```python
import jax
import jax.numpy as jnp
from jax import lax
from jax.experimental import pallas as pl
from jax.experimental.pallas import tpu as pltpu
from jax.sharding import Mesh
from jax.sharding import PartitionSpec as P

teleport = 0.2

USER_AXES = ("ylo", "x", "z")
PANEL_AXES = ("yhi", "core")


def block_sum_kernel(index_ref, a_ref, b_ref, o_ref, *, b_transposed):
    o_ref[...] = jnp.zeros(o_ref.shape, o_ref.dtype)
    n_blocks = index_ref.shape[0] // 3

    def body(k, carry):
        a = a_ref[index_ref[k]]
        b = b_ref[index_ref[n_blocks + k]]
        contract = ((1,), (1,) if b_transposed else (0,))
        o_ref[index_ref[2 * n_blocks + k]] += lax.dot_general(
            a, b, (contract, ((), ())), preferred_element_type=jnp.float32
        )
        return carry

    lax.fori_loop(0, n_blocks, body, 0, unroll=64)


def block_sums(index, a_tiles, b_tiles, n_out, b_transposed=False):
    import functools

    tile = a_tiles.shape[1]
    width = b_tiles.shape[1] if b_transposed else b_tiles.shape[2]
    return pl.pallas_call(
        functools.partial(block_sum_kernel, b_transposed=b_transposed),
        grid_spec=pltpu.PrefetchScalarGridSpec(
            num_scalar_prefetch=1,
            grid=(1,),
            in_specs=[
                pl.BlockSpec(a_tiles.shape, lambda i, *_: (0, 0, 0)),
                pl.BlockSpec(b_tiles.shape, lambda i, *_: (0, 0, 0)),
            ],
            out_specs=pl.BlockSpec((n_out, tile, width), lambda i, *_: (0, 0, 0)),
        ),
        out_shape=jax.ShapeDtypeStruct((n_out, tile, width), jnp.float32),
    )(index, a_tiles, b_tiles)


def ring_reduce_scatter(x, axis, n):
    h = x.shape[1] // 2
    return jnp.concatenate(ring_reduce_scatter_halves(x[:, :h], x[:, h:], axis, n), 0)


def ring_reduce_scatter_halves(xl, xr, axis, n):
    i = lax.axis_index(axis)
    right = [(j, (j + 1) % n) for j in range(n)]
    left = [(j, (j - 1) % n) for j in range(n)]
    bl = lax.dynamic_index_in_dim(xl, (i - 1) % n, 0, keepdims=False)
    br = lax.dynamic_index_in_dim(xr, (i + 1) % n, 0, keepdims=False)
    for s in range(n - 1):
        rl = lax.ppermute(bl, axis, right)
        rr = lax.ppermute(br, axis, left)
        bl = rl + lax.dynamic_index_in_dim(xl, (i - s - 2) % n, 0, keepdims=False)
        br = rr + lax.dynamic_index_in_dim(xr, (i + s + 2) % n, 0, keepdims=False)
    return bl, br


def ring_all_gather(x, axis, n):
    i = lax.axis_index(axis)
    h = x.shape[0] // 2
    right = [(j, (j + 1) % n) for j in range(n)]
    left = [(j, (j - 1) % n) for j in range(n)]
    out = jnp.zeros((n,) + x.shape, x.dtype)
    out = lax.dynamic_update_index_in_dim(out, x, i, 0)
    bl, br = x[:h], x[h:]
    zeros = (0,) * (x.ndim - 1)
    for s in range(n - 1):
        bl = lax.ppermute(bl, axis, right)
        br = lax.ppermute(br, axis, left)
        out = lax.dynamic_update_slice(out, bl[None], ((i - s - 1) % n, 0) + zeros)
        out = lax.dynamic_update_slice(out, br[None], ((i + s + 1) % n, h) + zeros)
    return out


def per_device(user_emb0, item_base, weight_tiles, blk_user, blk_item, blk_weight, *, sizes):
    n_ylo, n_x, n_z, n_yhi, n_core = sizes
    n_users = n_ylo * n_x * n_z
    tile_rows = weight_tiles.shape[1]
    width = user_emb0.shape[1]
    n_user_tiles = user_emb0.shape[0] // tile_rows
    user_tiles_t = jnp.swapaxes(user_emb0.astype(jnp.bfloat16).reshape(-1, tile_rows, width), 1, 2)
    users_list = blk_user.reshape(-1)
    items_list = blk_item.reshape(-1)
    weights_list = blk_weight.reshape(-1)

    item_ylo = items_list // (n_x * n_z)
    item_x = (items_list // n_z) % n_x
    item_z = items_list % n_z
    item_slot = (item_ylo * n_z + item_z) * n_x + item_x
    item_index = jnp.concatenate([users_list, weights_list, item_slot])
    partial_t = block_sums(item_index, user_tiles_t, weight_tiles, n_users)
    halves = partial_t.reshape(n_ylo, n_z, n_x * tile_rows, width)
    bl, br = ring_reduce_scatter_halves(halves[0], halves[1], "z", n_z)
    x = jnp.concatenate([bl, br], 0).reshape(n_ylo * n_x, tile_rows, width)
    x = lax.all_to_all(x, ("ylo", "x"), 0, 0, tiled=True)
    own_sum = x.sum(0).T

    position = lax.axis_index(USER_AXES)
    own_base = lax.dynamic_slice_in_dim(item_base[0], position * tile_rows, tile_rows, 0)
    own_emb = (1.0 - teleport) * own_sum + teleport * own_base
    own_bf = own_emb.astype(jnp.bfloat16)
    t = lax.all_to_all(jnp.broadcast_to(own_bf[None], (n_z, tile_rows, width)), "z", 0, 0, tiled=True)
    t = jnp.broadcast_to(t[None], (n_ylo * n_x, n_z, tile_rows, width))
    t = lax.all_to_all(t, ("ylo", "x"), 0, 0, tiled=True)
    item_tiles = t.reshape(n_users, tile_rows, width)

    user_index = jnp.concatenate([weights_list, items_list, users_list])
    user_part = block_sums(user_index, weight_tiles, item_tiles, n_user_tiles)
    y = user_part.reshape(-1, width)
    y = y + lax.ppermute(y, "core", [(j, (j + 1) % n_core) for j in range(n_core)])
    y = y + lax.ppermute(y, "yhi", [(j, (j + 1) % n_yhi) for j in range(n_yhi)])
    user_out = (1.0 - teleport) * y + teleport * user_emb0
    return (user_out, own_emb[None])


def solution(mesh):
    import functools

    sizes = (2, 4, 8, 2, 2)
    fine = Mesh(mesh.devices.reshape(sizes), USER_AXES + PANEL_AXES)
    placed = (
        P(USER_AXES, None),
        P(PANEL_AXES, None, None),
        P(),
        P(USER_AXES, PANEL_AXES, None),
        P(USER_AXES, PANEL_AXES, None),
        P(USER_AXES, PANEL_AXES, None),
    )
    return jax.shard_map(
        functools.partial(per_device, sizes=sizes),
        mesh=fine,
        in_specs=placed,
        out_specs=(P(USER_AXES, None), P(PANEL_AXES, USER_AXES, None)),
        check_vma=False,
    )
```

```python
import jax
import jax.numpy as jnp
from jax import lax
from jax.experimental import pallas as pl
from jax.experimental.pallas import tpu as pltpu
from jax.sharding import Mesh
from jax.sharding import PartitionSpec as P

teleport = 0.2

USER_AXES = ("ylo", "x", "z")
PANEL_AXES = ("yhi", "core")


def block_sum_kernel(index_ref, a_ref, b_ref, o_ref, *, b_transposed):
    o_ref[...] = jnp.zeros(o_ref.shape, o_ref.dtype)
    n_blocks = index_ref.shape[0] // 3

    def body(k, carry):
        a = a_ref[index_ref[k]]
        b = b_ref[index_ref[n_blocks + k]]
        contract = ((1,), (1,) if b_transposed else (0,))
        o_ref[index_ref[2 * n_blocks + k]] += lax.dot_general(
            a, b, (contract, ((), ())), preferred_element_type=jnp.float32
        )
        return carry

    lax.fori_loop(0, n_blocks, body, 0, unroll=64)


def block_sums(index, a_tiles, b_tiles, n_out, b_transposed=False):
    import functools

    tile = a_tiles.shape[1]
    width = b_tiles.shape[1] if b_transposed else b_tiles.shape[2]
    return pl.pallas_call(
        functools.partial(block_sum_kernel, b_transposed=b_transposed),
        grid_spec=pltpu.PrefetchScalarGridSpec(
            num_scalar_prefetch=1,
            grid=(1,),
            in_specs=[
                pl.BlockSpec(a_tiles.shape, lambda i, *_: (0, 0, 0)),
                pl.BlockSpec(b_tiles.shape, lambda i, *_: (0, 0, 0)),
            ],
            out_specs=pl.BlockSpec((n_out, tile, width), lambda i, *_: (0, 0, 0)),
        ),
        out_shape=jax.ShapeDtypeStruct((n_out, tile, width), jnp.float32),
    )(index, a_tiles, b_tiles)


def ring_reduce_scatter(x, axis, n):
    h = x.shape[1] // 2
    return jnp.concatenate(ring_reduce_scatter_halves(x[:, :h], x[:, h:], axis, n), 0)


def ring_reduce_scatter_halves(xl, xr, axis, n):
    i = lax.axis_index(axis)
    right = [(j, (j + 1) % n) for j in range(n)]
    left = [(j, (j - 1) % n) for j in range(n)]
    bl = lax.dynamic_index_in_dim(xl, (i - 1) % n, 0, keepdims=False)
    br = lax.dynamic_index_in_dim(xr, (i + 1) % n, 0, keepdims=False)
    for s in range(n - 1):
        rl = lax.ppermute(bl, axis, right)
        rr = lax.ppermute(br, axis, left)
        bl = rl + lax.dynamic_index_in_dim(xl, (i - s - 2) % n, 0, keepdims=False)
        br = rr + lax.dynamic_index_in_dim(xr, (i + s + 2) % n, 0, keepdims=False)
    return bl, br


def ring_all_gather(x, axis, n):
    i = lax.axis_index(axis)
    h = x.shape[0] // 2
    right = [(j, (j + 1) % n) for j in range(n)]
    left = [(j, (j - 1) % n) for j in range(n)]
    out = jnp.zeros((n,) + x.shape, x.dtype)
    out = lax.dynamic_update_index_in_dim(out, x, i, 0)
    bl, br = x[:h], x[h:]
    zeros = (0,) * (x.ndim - 1)
    for s in range(n - 1):
        bl = lax.ppermute(bl, axis, right)
        br = lax.ppermute(br, axis, left)
        out = lax.dynamic_update_slice(out, bl[None], ((i - s - 1) % n, 0) + zeros)
        out = lax.dynamic_update_slice(out, br[None], ((i + s + 1) % n, h) + zeros)
    return out


def per_device(user_emb0, item_base, weight_tiles, blk_user, blk_item, blk_weight, *, sizes):
    n_ylo, n_x, n_z, n_yhi, n_core = sizes
    n_users = n_ylo * n_x * n_z
    tile_rows = weight_tiles.shape[1]
    width = user_emb0.shape[1]
    n_user_tiles = user_emb0.shape[0] // tile_rows
    user_tiles_t = jnp.swapaxes(user_emb0.astype(jnp.bfloat16).reshape(-1, tile_rows, width), 1, 2)
    users_list = blk_user.reshape(-1)
    items_list = blk_item.reshape(-1)
    weights_list = blk_weight.reshape(-1)

    item_ylo = items_list // (n_x * n_z)
    item_x = (items_list // n_z) % n_x
    item_z = items_list % n_z
    item_slot = (item_ylo * n_z + item_z) * n_x + item_x
    item_index = jnp.concatenate([users_list, weights_list, item_slot])
    partial_t = block_sums(item_index, user_tiles_t, weight_tiles, n_users)
    halves = partial_t.reshape(n_ylo, n_z, n_x * tile_rows, width)
    bl, br = ring_reduce_scatter_halves(halves[0], halves[1], "z", n_z)
    x = jnp.concatenate([bl, br], 0).reshape(n_ylo * n_x, tile_rows, width)
    x = lax.all_to_all(x, ("ylo", "x"), 0, 0, tiled=True)
    own_sum = x.sum(0).T

    position = lax.axis_index(USER_AXES)
    own_base = lax.dynamic_slice_in_dim(item_base[0], position * tile_rows, tile_rows, 0)
    own_emb = (1.0 - teleport) * own_sum + teleport * own_base
    own_bf = own_emb.astype(jnp.bfloat16)
    t = own_bf[None]
    z_index = lax.axis_index("z")
    step = 1
    while step < n_z:
        other = lax.ppermute(t, "z", [(j, j ^ step) for j in range(n_z)])
        low = (z_index // step) % 2 == 0
        t = jnp.where(low, jnp.concatenate([t, other], 0), jnp.concatenate([other, t], 0))
        step *= 2
    t = jnp.broadcast_to(t[None], (n_ylo * n_x, n_z, tile_rows, width))
    t = lax.all_to_all(t, ("ylo", "x"), 0, 0, tiled=True)
    item_tiles = t.reshape(n_users, tile_rows, width)

    user_index = jnp.concatenate([weights_list, items_list, users_list])
    user_part = block_sums(user_index, weight_tiles, item_tiles, n_user_tiles)
    y = user_part.reshape(-1, width)
    y = y + lax.ppermute(y, "core", [(j, (j + 1) % n_core) for j in range(n_core)])
    y = y + lax.ppermute(y, "yhi", [(j, (j + 1) % n_yhi) for j in range(n_yhi)])
    user_out = (1.0 - teleport) * y + teleport * user_emb0
    return (user_out, own_emb[None])


def solution(mesh):
    import functools

    sizes = (2, 4, 8, 2, 2)
    fine = Mesh(mesh.devices.reshape(sizes), USER_AXES + PANEL_AXES)
    placed = (
        P(USER_AXES, None),
        P(PANEL_AXES, None, None),
        P(),
        P(USER_AXES, PANEL_AXES, None),
        P(USER_AXES, PANEL_AXES, None),
        P(USER_AXES, PANEL_AXES, None),
    )
    return jax.shard_map(
        functools.partial(per_device, sizes=sizes),
        mesh=fine,
        in_specs=placed,
        out_specs=(P(USER_AXES, None), P(PANEL_AXES, USER_AXES, None)),
        check_vma=False,
    )
```

```python
import jax
import jax.numpy as jnp
from jax import lax
from jax.experimental import pallas as pl
from jax.experimental.pallas import tpu as pltpu
from jax.sharding import Mesh
from jax.sharding import PartitionSpec as P

teleport = 0.2

USER_AXES = ("ylo", "x", "z")
PANEL_AXES = ("yhi", "core")


def block_sum_kernel(index_ref, a_ref, b_ref, o_ref, *, b_transposed):
    o_ref[...] = jnp.zeros(o_ref.shape, o_ref.dtype)
    n_blocks = index_ref.shape[0] // 3

    def body(k, carry):
        a = a_ref[index_ref[k]]
        b = b_ref[index_ref[n_blocks + k]]
        contract = ((1,), (1,) if b_transposed else (0,))
        o_ref[index_ref[2 * n_blocks + k]] += lax.dot_general(
            a, b, (contract, ((), ())), preferred_element_type=jnp.float32
        )
        return carry

    lax.fori_loop(0, n_blocks, body, 0, unroll=64)


def block_sums(index, a_tiles, b_tiles, n_out, b_transposed=False):
    import functools

    tile = a_tiles.shape[1]
    width = b_tiles.shape[1] if b_transposed else b_tiles.shape[2]
    return pl.pallas_call(
        functools.partial(block_sum_kernel, b_transposed=b_transposed),
        grid_spec=pltpu.PrefetchScalarGridSpec(
            num_scalar_prefetch=1,
            grid=(1,),
            in_specs=[
                pl.BlockSpec(a_tiles.shape, lambda i, *_: (0, 0, 0)),
                pl.BlockSpec(b_tiles.shape, lambda i, *_: (0, 0, 0)),
            ],
            out_specs=pl.BlockSpec((n_out, tile, width), lambda i, *_: (0, 0, 0)),
        ),
        out_shape=jax.ShapeDtypeStruct((n_out, tile, width), jnp.float32),
    )(index, a_tiles, b_tiles)


def ring_reduce_scatter(x, axis, n):
    h = x.shape[1] // 2
    return jnp.concatenate(ring_reduce_scatter_halves(x[:, :h], x[:, h:], axis, n), 0)


def ring_reduce_scatter_halves(xl, xr, axis, n):
    i = lax.axis_index(axis)
    right = [(j, (j + 1) % n) for j in range(n)]
    left = [(j, (j - 1) % n) for j in range(n)]
    bl = lax.dynamic_index_in_dim(xl, (i - 1) % n, 0, keepdims=False)
    br = lax.dynamic_index_in_dim(xr, (i + 1) % n, 0, keepdims=False)
    for s in range(n - 1):
        rl = lax.ppermute(bl, axis, right)
        rr = lax.ppermute(br, axis, left)
        bl = rl + lax.dynamic_index_in_dim(xl, (i - s - 2) % n, 0, keepdims=False)
        br = rr + lax.dynamic_index_in_dim(xr, (i + s + 2) % n, 0, keepdims=False)
    return bl, br


def ring_all_gather(x, axis, n):
    i = lax.axis_index(axis)
    h = x.shape[0] // 2
    right = [(j, (j + 1) % n) for j in range(n)]
    left = [(j, (j - 1) % n) for j in range(n)]
    out = jnp.zeros((n,) + x.shape, x.dtype)
    out = lax.dynamic_update_index_in_dim(out, x, i, 0)
    bl, br = x[:h], x[h:]
    zeros = (0,) * (x.ndim - 1)
    for s in range(n - 1):
        bl = lax.ppermute(bl, axis, right)
        br = lax.ppermute(br, axis, left)
        out = lax.dynamic_update_slice(out, bl[None], ((i - s - 1) % n, 0) + zeros)
        out = lax.dynamic_update_slice(out, br[None], ((i + s + 1) % n, h) + zeros)
    return out


def per_device(user_emb0, item_base, weight_tiles, blk_user, blk_item, blk_weight, *, sizes):
    n_ylo, n_x, n_z, n_yhi, n_core = sizes
    n_users = n_ylo * n_x * n_z
    tile_rows = weight_tiles.shape[1]
    width = user_emb0.shape[1]
    n_user_tiles = user_emb0.shape[0] // tile_rows
    user_tiles_t = jnp.swapaxes(user_emb0.astype(jnp.bfloat16).reshape(-1, tile_rows, width), 1, 2)
    users_list = blk_user.reshape(-1)
    items_list = blk_item.reshape(-1)
    weights_list = blk_weight.reshape(-1)

    item_ylo = items_list // (n_x * n_z)
    item_x = (items_list // n_z) % n_x
    item_z = items_list % n_z
    item_slot = (item_ylo * n_z + item_z) * n_x + item_x
    item_index = jnp.concatenate([users_list, weights_list, item_slot])
    partial_t = block_sums(item_index, user_tiles_t, weight_tiles, n_users)
    halves = partial_t.reshape(n_ylo, n_z, n_x * tile_rows, width)
    bl, br = ring_reduce_scatter_halves(halves[0], halves[1], "z", n_z)
    low = lax.axis_index("ylo") == 0
    keep = jnp.where(low, bl, br)
    send = jnp.where(low, br, bl)
    x = keep + lax.ppermute(send, "ylo", [(j, (j + 1) % n_ylo) for j in range(n_ylo)])
    x = lax.all_to_all(x.reshape(n_x, tile_rows, width), "x", 0, 0, tiled=True)
    own_sum = x.sum(0).T

    position = lax.axis_index(USER_AXES)
    own_base = lax.dynamic_slice_in_dim(item_base[0], position * tile_rows, tile_rows, 0)
    own_emb = (1.0 - teleport) * own_sum + teleport * own_base
    own_bf = own_emb.astype(jnp.bfloat16)
    t = lax.all_to_all(jnp.broadcast_to(own_bf[None], (n_z, tile_rows, width)), "z", 0, 0, tiled=True)
    t = jnp.broadcast_to(t[None], (n_ylo * n_x, n_z, tile_rows, width))
    t = lax.all_to_all(t, ("ylo", "x"), 0, 0, tiled=True)
    item_tiles = t.reshape(n_users, tile_rows, width)

    user_index = jnp.concatenate([weights_list, items_list, users_list])
    user_part = block_sums(user_index, weight_tiles, item_tiles, n_user_tiles)
    y = user_part.reshape(-1, width)
    y = y + lax.ppermute(y, "core", [(j, (j + 1) % n_core) for j in range(n_core)])
    y = y + lax.ppermute(y, "yhi", [(j, (j + 1) % n_yhi) for j in range(n_yhi)])
    user_out = (1.0 - teleport) * y + teleport * user_emb0
    return (user_out, own_emb[None])


def solution(mesh):
    import functools

    sizes = (2, 4, 8, 2, 2)
    fine = Mesh(mesh.devices.reshape(sizes), USER_AXES + PANEL_AXES)
    placed = (
        P(USER_AXES, None),
        P(PANEL_AXES, None, None),
        P(),
        P(USER_AXES, PANEL_AXES, None),
        P(USER_AXES, PANEL_AXES, None),
        P(USER_AXES, PANEL_AXES, None),
    )
    return jax.shard_map(
        functools.partial(per_device, sizes=sizes),
        mesh=fine,
        in_specs=placed,
        out_specs=(P(USER_AXES, None), P(PANEL_AXES, USER_AXES, None)),
        check_vma=False,
    )
```

```python
import jax
import jax.numpy as jnp
from jax import lax
from jax.experimental import pallas as pl
from jax.experimental.pallas import tpu as pltpu
from jax.sharding import Mesh
from jax.sharding import PartitionSpec as P

teleport = 0.2

USER_AXES = ("ylo", "x", "z")
PANEL_AXES = ("yhi", "core")


def block_sum_kernel(index_ref, a_ref, b_ref, o_ref, *, b_transposed):
    o_ref[...] = jnp.zeros(o_ref.shape, o_ref.dtype)
    n_blocks = index_ref.shape[0] // 3

    def body(k, carry):
        a = a_ref[index_ref[k]]
        b = b_ref[index_ref[n_blocks + k]]
        contract = ((1,), (1,) if b_transposed else (0,))
        o_ref[index_ref[2 * n_blocks + k]] += lax.dot_general(
            a, b, (contract, ((), ())), preferred_element_type=jnp.float32
        )
        return carry

    lax.fori_loop(0, n_blocks, body, 0, unroll=128)


def block_sums(index, a_tiles, b_tiles, n_out, b_transposed=False):
    import functools

    tile = a_tiles.shape[1]
    width = b_tiles.shape[1] if b_transposed else b_tiles.shape[2]
    return pl.pallas_call(
        functools.partial(block_sum_kernel, b_transposed=b_transposed),
        grid_spec=pltpu.PrefetchScalarGridSpec(
            num_scalar_prefetch=1,
            grid=(1,),
            in_specs=[
                pl.BlockSpec(a_tiles.shape, lambda i, *_: (0, 0, 0)),
                pl.BlockSpec(b_tiles.shape, lambda i, *_: (0, 0, 0)),
            ],
            out_specs=pl.BlockSpec((n_out, tile, width), lambda i, *_: (0, 0, 0)),
        ),
        out_shape=jax.ShapeDtypeStruct((n_out, tile, width), jnp.float32),
    )(index, a_tiles, b_tiles)


def ring_reduce_scatter(x, axis, n):
    h = x.shape[1] // 2
    return jnp.concatenate(ring_reduce_scatter_halves(x[:, :h], x[:, h:], axis, n), 0)


def ring_reduce_scatter_halves(xl, xr, axis, n):
    i = lax.axis_index(axis)
    right = [(j, (j + 1) % n) for j in range(n)]
    left = [(j, (j - 1) % n) for j in range(n)]
    bl = lax.dynamic_index_in_dim(xl, (i - 1) % n, 0, keepdims=False)
    br = lax.dynamic_index_in_dim(xr, (i + 1) % n, 0, keepdims=False)
    for s in range(n - 1):
        rl = lax.ppermute(bl, axis, right)
        rr = lax.ppermute(br, axis, left)
        bl = rl + lax.dynamic_index_in_dim(xl, (i - s - 2) % n, 0, keepdims=False)
        br = rr + lax.dynamic_index_in_dim(xr, (i + s + 2) % n, 0, keepdims=False)
    return bl, br


def ring_all_gather(x, axis, n):
    i = lax.axis_index(axis)
    h = x.shape[0] // 2
    right = [(j, (j + 1) % n) for j in range(n)]
    left = [(j, (j - 1) % n) for j in range(n)]
    out = jnp.zeros((n,) + x.shape, x.dtype)
    out = lax.dynamic_update_index_in_dim(out, x, i, 0)
    bl, br = x[:h], x[h:]
    zeros = (0,) * (x.ndim - 1)
    for s in range(n - 1):
        bl = lax.ppermute(bl, axis, right)
        br = lax.ppermute(br, axis, left)
        out = lax.dynamic_update_slice(out, bl[None], ((i - s - 1) % n, 0) + zeros)
        out = lax.dynamic_update_slice(out, br[None], ((i + s + 1) % n, h) + zeros)
    return out


def per_device(user_emb0, item_base, weight_tiles, blk_user, blk_item, blk_weight, *, sizes):
    n_ylo, n_x, n_z, n_yhi, n_core = sizes
    n_users = n_ylo * n_x * n_z
    tile_rows = weight_tiles.shape[1]
    width = user_emb0.shape[1]
    n_user_tiles = user_emb0.shape[0] // tile_rows
    user_tiles_t = jnp.swapaxes(user_emb0.astype(jnp.bfloat16).reshape(-1, tile_rows, width), 1, 2)
    users_list = blk_user.reshape(-1)
    items_list = blk_item.reshape(-1)
    weights_list = blk_weight.reshape(-1)

    item_ylo = items_list // (n_x * n_z)
    item_x = (items_list // n_z) % n_x
    item_z = items_list % n_z
    item_slot = (item_ylo * n_z + item_z) * n_x + item_x
    item_index = jnp.concatenate([users_list, weights_list, item_slot])
    partial_t = block_sums(item_index, user_tiles_t, weight_tiles, n_users)
    halves = partial_t.reshape(n_ylo, n_z, n_x * tile_rows, width)
    bl, br = ring_reduce_scatter_halves(halves[0], halves[1], "z", n_z)
    x = jnp.concatenate([bl, br], 0).reshape(n_ylo * n_x, tile_rows, width)
    x = lax.all_to_all(x, ("ylo", "x"), 0, 0, tiled=True)
    own_sum = x.sum(0).T

    position = lax.axis_index(USER_AXES)
    own_base = lax.dynamic_slice_in_dim(item_base[0], position * tile_rows, tile_rows, 0)
    own_emb = (1.0 - teleport) * own_sum + teleport * own_base
    own_bf = own_emb.astype(jnp.bfloat16)
    t = lax.all_to_all(jnp.broadcast_to(own_bf[None], (n_z, tile_rows, width)), "z", 0, 0, tiled=True)
    t = jnp.broadcast_to(t[None], (n_ylo * n_x, n_z, tile_rows, width))
    t = lax.all_to_all(t, ("ylo", "x"), 0, 0, tiled=True)
    item_tiles = t.reshape(n_users, tile_rows, width)

    user_index = jnp.concatenate([weights_list, items_list, users_list])
    user_part = block_sums(user_index, weight_tiles, item_tiles, n_user_tiles)
    y = user_part.reshape(-1, width)
    y = y + lax.ppermute(y, "core", [(j, (j + 1) % n_core) for j in range(n_core)])
    y = y + lax.ppermute(y, "yhi", [(j, (j + 1) % n_yhi) for j in range(n_yhi)])
    user_out = (1.0 - teleport) * y + teleport * user_emb0
    return (user_out, own_emb[None])


def solution(mesh):
    import functools

    sizes = (2, 4, 8, 2, 2)
    fine = Mesh(mesh.devices.reshape(sizes), USER_AXES + PANEL_AXES)
    placed = (
        P(USER_AXES, None),
        P(PANEL_AXES, None, None),
        P(),
        P(USER_AXES, PANEL_AXES, None),
        P(USER_AXES, PANEL_AXES, None),
        P(USER_AXES, PANEL_AXES, None),
    )
    return jax.shard_map(
        functools.partial(per_device, sizes=sizes),
        mesh=fine,
        in_specs=placed,
        out_specs=(P(USER_AXES, None), P(PANEL_AXES, USER_AXES, None)),
        check_vma=False,
    )
```
